32 devices in a mesh: seq: 16 (over z, y, core), tp: 2 (over x).
Axes of the slice: x: 2, y: 2, z: 4, core: 2. Of those that a mesh axis runs over, the one named last changes fastest.
Arguments:
- hidden: bfloat16 [1920, 5120], P(('seq', 'tp')), may hold values from -6 to 6
- queries: bfloat16 [1920, 2560], P('seq', 'tp'), may hold values from -10 to 10
- key_rows: bfloat16 [1920, 2560], P('seq', 'tp'), may hold values from -10 to 10
- value_rows: bfloat16 [1920, 2560], P('seq', 'tp'), may hold values from -6 to 6
- gate_scale: float32 [5120], replicated, may hold values from 0.5 to 2
- out_weight: bfloat16 [2560, 5120], P('tp'), may hold values from -0.125 to 0.125
- valid_count: int32 [16], P('seq'), may hold values from 1 to 120, 1200 in all
- assignment: int32 [16], P('seq'), may hold values from 0 to 15, each once
Outputs:
- mixed: bfloat16 [1920, 5120], P(('seq', 'tp'))
The draws below stay inside these ranges and needn't reach their ends.
All inputs are finite; a program needn't handle non-finite values. No bound on the sum of `valid_count` on one device may be relied on, other than what follows from the above.
Results may differ from the reference program's by a relative error of at most 0.0075.
Values may be sent and summed in bfloat16 or wider, within the bound.
No kernel may reach another device: no remote copies, remote signals or barrier semaphores. Data moves between devices by JAX's collectives and lax.ppermute only.
A program may use at most 192 MiB of HBM per device.

```python
import math
import jax
import jax.numpy as jnp
import numpy as np
from jax import lax

D = 5120
HEADS = 20
HEAD = 128
TOK_DEV = 120
TOKENS = 1920
N_SEQ = 16


def drawn_pair(key):
    base_key = jax.random.fold_in(key, 71)
    width = HEADS * HEAD
    query_vals = 1.5 * jax.random.truncated_normal(jax.random.fold_in(base_key, 1), -5.0, 5.0, (TOKENS, width), jnp.float32)
    key_vals = 1.5 * jax.random.truncated_normal(jax.random.fold_in(base_key, 2), -5.0, 5.0, (TOKENS, width), jnp.float32)
    return (query_vals, key_vals)


def draw_queries(key, part):
    query_vals, key_vals = drawn_pair(key)
    return query_vals.astype(jnp.bfloat16)


def draw_key_rows(key, part):
    query_vals, key_vals = drawn_pair(key)
    return key_vals.astype(jnp.bfloat16)


def shard_levels(key, dims, cuts, low, high):
    loudness, own = 1.0, jax.random.fold_in(key, 6)
    for axis_at, blocks in cuts:
        draws = jnp.exp(jax.random.uniform(jax.random.fold_in(own, axis_at), (blocks,), jnp.float32, low / len(cuts), high / len(cuts)))
        loudness = loudness * jnp.repeat(draws, dims[axis_at] // blocks).reshape([-1 if axis == axis_at else 1 for axis in range(len(dims))])
    return loudness


def split_up(number_of, total, reach, skew):
    loads = [(1 << 20) // math.isqrt(rank ** skew) + 1 for rank in range(2, number_of + 1)]
    surplus, counts = total - reach - (number_of - 1), [1] * (number_of - 1)
    while surplus > 0:
        free = [i for i in range(number_of - 1) if counts[i] < reach]
        pool, remaining = sum([loads[i] for i in free]), surplus
        for i in free:
            extra = min(reach - counts[i], max(1, remaining * loads[i] // pool), surplus)
            counts[i] = counts[i] + extra
            surplus = surplus - extra
    return np.array([reach] + counts)


def uneven(key, amount, total, reach, lean):
    if amount == 2:
        one = jax.random.randint(key, (), max(1, total - reach), min(reach, total - 1) + 1)
        return jnp.stack([one, total - one])
    lengths = jnp.asarray(split_up(amount, total, reach, lean), jnp.int32)
    twos = (amount - 1) // 2
    giver, taker = lengths[1:1 + 2 * twos:2], lengths[2:2 + 2 * twos:2]
    slack = jnp.minimum(giver - 1, reach - taker)
    moved = jax.random.randint(jax.random.fold_in(key, 1), (twos,), 0, 1 << 20) % (slack + 1)
    lengths = lengths.at[1:1 + 2 * twos:2].set(giver - moved).at[2:2 + 2 * twos:2].set(taker + moved)
    return lengths[jax.random.permutation(jax.random.fold_in(key, 2), amount)]


def noise(stream_key, extent, deviation, reach, split=(), kind=jnp.bfloat16):
    array = jax.random.normal(stream_key, extent, jnp.float32) * deviation
    if len(split) > 0:
        array = shard_levels(stream_key, extent, split, -0.22, 0.18) * array
    return jnp.clip(array, min=-reach, max=reach).astype(kind)


def setup_inputs(seed: int = 0) -> dict:
    key_list = jax.random.split(jax.random.key(seed), 9)
    hidden = noise(key_list[0], (TOKENS, D), 0.5, 6.0, ((0, 32),))
    queries = draw_queries(jax.random.fold_in(key_list[8], 71), 0)
    key_rows = draw_key_rows(jax.random.fold_in(key_list[8], 71), 0)
    value_rows = noise(key_list[3], (TOKENS, HEADS * HEAD), 1.0, 6.0, ((0, 16), (1, 2)))
    gate_scale = jnp.clip(jax.random.uniform(key_list[4], (D,), jnp.float32, 0.5, 2.0), 0.5, 2.0)
    out_weight = noise(key_list[5], (HEADS * HEAD, D), (HEADS * HEAD) ** -0.5, 0.125, ((0, 2),))
    valid_count = uneven(key_list[6], N_SEQ, TOKENS * 5 // 8, TOK_DEV, 2).astype(jnp.int32)
    assignment = jax.random.permutation(key_list[7], N_SEQ).astype(jnp.int32)
    return dict(hidden=hidden, queries=queries, key_rows=key_rows, value_rows=value_rows, gate_scale=gate_scale, out_weight=out_weight, valid_count=valid_count, assignment=assignment)


def reference(hidden, queries, key_rows, value_rows, gate_scale, out_weight, valid_count, assignment):
    tokens_all = queries.shape[0]
    blocks = tokens_all // TOK_DEV
    positions = jnp.arange(tokens_all, dtype=jnp.int32)
    holder = positions // TOK_DEV
    within = positions % TOK_DEV
    kept = within < valid_count[assignment[holder]]
    scale_factor = 1.0 / math.sqrt(HEAD)
    stacked_q = queries.reshape(blocks, TOK_DEV, HEADS, HEAD).transpose(2, 0, 1, 3)
    stacked_k = key_rows.reshape(tokens_all, HEADS, HEAD).transpose(1, 0, 2)
    stacked_v = value_rows.reshape(tokens_all, HEADS, HEAD).transpose(1, 0, 2)

    def one_head(operands):
        head_q, head_k, head_v = operands

        def one_block(block_q):
            scores = jnp.dot(block_q, head_k.T, preferred_element_type=jnp.float32) * scale_factor
            masked = jnp.where(kept[None, :], scores, -1e+30)
            peak = lax.optimization_barrier(jnp.max(masked, axis=1, keepdims=True))
            weights = jnp.where(kept[None, :], jnp.exp(masked - peak), 0.0)
            totals = lax.optimization_barrier(jnp.sum(weights, axis=1, keepdims=True))
            rounded = weights.astype(jnp.bfloat16)
            summed = jnp.dot(rounded, head_v, preferred_element_type=jnp.float32)
            return (summed / totals).astype(jnp.bfloat16)
        return lax.map(one_block, head_q).reshape(tokens_all, HEAD)
    heads_out = lax.map(one_head, (stacked_q, stacked_k, stacked_v))
    attention = heads_out.transpose(1, 0, 2).reshape(tokens_all, HEADS * HEAD)
    projected = jnp.dot(attention, out_weight, preferred_element_type=jnp.float32)
    return (hidden.astype(jnp.float32) + gate_scale * projected).astype(jnp.bfloat16)
```

```python
import math

import jax
import jax.numpy as jnp
from jax import lax
from jax.sharding import PartitionSpec as P

HEAD = 128
neg_large = -1e30


def snake_ring(chips):
    half = chips // 2
    return [2 * a for a in range(half)] + [2 * a + 1 for a in reversed(range(half))]


def build(n_seq):
    chips = n_seq // 2
    ring = snake_ring(chips)
    place = [0] * chips
    for pos, chip in enumerate(ring):
        place[chip] = pos
    forward = [(ring[p] * 2 + c, ring[(p + 1) % chips] * 2 + c) for p in range(chips) for c in range(2)]
    backward = [(ring[(p + 1) % chips] * 2 + c, ring[p] * 2 + c) for p in range(chips) for c in range(2)]
    swap = [(i, i ^ 1) for i in range(n_seq)]
    ring_arr = jnp.asarray(ring, jnp.int32)
    place_arr = jnp.asarray(place, jnp.int32)

    def gather_ring(packet_a, packet_b, me):
        chip = me // 2
        core = me % 2
        pos = place_arr[chip]
        got_a, got_b, ids_a, ids_b = [], [], [], []
        cur_a, cur_b = packet_a, packet_b
        for step in range(chips):
            if step > 0:
                cur_a = lax.ppermute(cur_a, "seq", forward)
                cur_b = lax.ppermute(cur_b, "seq", backward)
            src_a = ring_arr[(pos - step) % chips] * 2 + core
            src_b = ring_arr[(pos + step) % chips] * 2 + core
            mate_a = lax.ppermute(cur_a, "seq", swap)
            mate_b = lax.ppermute(cur_b, "seq", swap)
            got_a += [cur_a, mate_a]
            got_b += [cur_b, mate_b]
            ids_a += [src_a, src_a ^ 1]
            ids_b += [src_b, src_b ^ 1]
        return got_a, got_b, jnp.stack(ids_a), jnp.stack(ids_b)

    return gather_ring


def attend_all(queries_3d, keys, values, keeping, scale_factor):
    scores = (
        jnp.einsum("qhd,khd->hqk", queries_3d, keys, preferred_element_type=jnp.float32)
        * scale_factor
    )
    masked = jnp.where(keeping[None, None, :], scores, neg_large)
    peak = jnp.max(masked, axis=2, keepdims=True)
    weights = jnp.where(keeping[None, None, :], jnp.exp(masked - peak), 0.0)
    totals = jnp.sum(weights, axis=2, keepdims=True)
    summed = jnp.einsum(
        "hqk,khd->hqd", weights.astype(jnp.bfloat16), values, preferred_element_type=jnp.float32
    )
    result = (summed / totals).astype(jnp.bfloat16)
    return result.transpose(1, 0, 2).reshape(queries_3d.shape[0], -1)


def solution(mesh):
    n_seq = mesh.shape["seq"]
    gather_ring = build(n_seq)

    def on_device(
        hidden, queries, key_rows, value_rows, gate_scale, out_weight, valid_count, assignment
    ):
        rows_dev = queries.shape[0]
        heads_here = queries.shape[1] // HEAD
        heads_a = heads_here // 2
        cut = heads_a * HEAD
        scale_factor = 1.0 / math.sqrt(HEAD)
        me = lax.axis_index("seq")
        pairs = lax.all_gather(jnp.concatenate([valid_count, assignment]), "seq", axis=0, tiled=False)
        counts_all, blocks_all = pairs[:, 0], pairs[:, 1]
        columns = jnp.arange(n_seq, dtype=jnp.int32)
        dev_counts = jnp.sum(
            jnp.where(blocks_all[:, None] == columns[None, :], counts_all[None, :], 0), axis=1
        )

        packet_a = jnp.concatenate([key_rows[:, :cut], value_rows[:, :cut]], axis=1)
        packet_b = jnp.concatenate([key_rows[:, cut:], value_rows[:, cut:]], axis=1)
        got_a, got_b, ids_a, ids_b = gather_ring(packet_a, packet_b, me)
        within = jnp.arange(rows_dev, dtype=jnp.int32)

        def half(got, ids, lo, hi):
            width = (hi - lo) * HEAD
            stack = jnp.concatenate(got, axis=0)
            keys = stack[:, :width].reshape(-1, hi - lo, HEAD)
            values = stack[:, width:].reshape(-1, hi - lo, HEAD)
            limits = jnp.sum(
                jnp.where(ids[:, None] == columns[None, :], dev_counts[None, :], 0), axis=1
            )
            keeping = (within[None, :] < limits[:, None]).reshape(-1)
            q3 = queries[:, lo * HEAD : hi * HEAD].reshape(rows_dev, hi - lo, HEAD)
            return attend_all(q3, keys, values, keeping, scale_factor)

        attention = jnp.concatenate(
            [half(got_a, ids_a, 0, heads_a), half(got_b, ids_b, heads_a, heads_here)], axis=1
        )
        partial = jnp.dot(attention, out_weight, preferred_element_type=jnp.float32)
        rows_out = hidden.shape[0]
        side = lax.axis_index("tp")
        n_tp = rows_dev // rows_out
        pieces = partial.reshape(n_tp, rows_out, partial.shape[1])
        own = jnp.take(pieces, side, axis=0)
        other = jnp.take(pieces, 1 - side, axis=0).astype(jnp.bfloat16)
        came = lax.ppermute(other, "tp", [(0, 1), (1, 0)])
        summed = own + came.astype(jnp.float32)
        return (hidden.astype(jnp.float32) + gate_scale * summed).astype(jnp.bfloat16)

    placed = (
        P(("seq", "tp"), None),
        P("seq", "tp"),
        P("seq", "tp"),
        P("seq", "tp"),
        P(),
        P("tp", None),
        P("seq"),
        P("seq"),
    )
    return jax.shard_map(
        on_device, mesh=mesh, in_specs=placed, out_specs=P(("seq", "tp"), None), check_vma=False
    )
```

```python
import math

import jax
import jax.numpy as jnp
from jax import lax
from jax.sharding import PartitionSpec as P

HEAD = 128
neg_large = -1e30


def snake_ring(chips):
    half = chips // 2
    return [2 * a for a in range(half)] + [2 * a + 1 for a in reversed(range(half))]


def build(n_seq):
    chips = n_seq // 2
    ring = snake_ring(chips)
    half = chips // 2
    forward = [(ring[p] * 2 + c, ring[(p + 1) % chips] * 2 + c) for p in range(chips) for c in range(2)]
    backward = [(ring[(p + 1) % chips] * 2 + c, ring[p] * 2 + c) for p in range(chips) for c in range(2)]
    swap = [(i, i ^ 1) for i in range(n_seq)]

    def chip_at(pos):
        return jnp.where(pos < half, 2 * pos, 2 * (chips - 1 - pos) + 1)

    def gather_ring(packet_a, packet_b, me):
        chip = me // 2
        core = me % 2
        pos = jnp.where(chip % 2 == 0, chip // 2, chips - 1 - chip // 2)
        got_a, got_b, ids_a, ids_b = [], [], [], []
        cur_a, cur_b = packet_a, packet_b
        for step in range(chips):
            if step > 0:
                cur_a = lax.ppermute(cur_a, "seq", forward)
                cur_b = lax.ppermute(cur_b, "seq", backward)
            src_a = chip_at((pos - step) % chips) * 2 + core
            src_b = chip_at((pos + step) % chips) * 2 + core
            mate_a = lax.ppermute(cur_a, "seq", swap)
            mate_b = lax.ppermute(cur_b, "seq", swap)
            got_a += [cur_a, mate_a]
            got_b += [cur_b, mate_b]
            ids_a += [src_a, src_a ^ 1]
            ids_b += [src_b, src_b ^ 1]
        return got_a, got_b, jnp.stack(ids_a), jnp.stack(ids_b)

    return gather_ring


def attend_all(queries_3d, keys, values, keeping, scale_factor):
    scores = (
        jnp.einsum("qhd,khd->hqk", queries_3d, keys, preferred_element_type=jnp.float32)
        * scale_factor
    )
    masked = jnp.where(keeping[None, None, :], scores, neg_large)
    peak = jnp.max(masked, axis=2, keepdims=True)
    weights = jnp.where(keeping[None, None, :], jnp.exp(masked - peak), 0.0)
    totals = jnp.sum(weights, axis=2, keepdims=True)
    summed = jnp.einsum(
        "hqk,khd->hqd", weights.astype(jnp.bfloat16), values, preferred_element_type=jnp.float32
    )
    result = (summed / totals).astype(jnp.bfloat16)
    return result.transpose(1, 0, 2).reshape(queries_3d.shape[0], -1)


def solution(mesh):
    n_seq = mesh.shape["seq"]
    gather_ring = build(n_seq)

    def on_device(
        hidden, queries, key_rows, value_rows, gate_scale, out_weight, valid_count, assignment
    ):
        rows_dev = queries.shape[0]
        heads_here = queries.shape[1] // HEAD
        heads_a = heads_here // 2
        cut = heads_a * HEAD
        scale_factor = 1.0 / math.sqrt(HEAD)
        me = lax.axis_index("seq")
        info = jnp.zeros((1, 2 * cut), jnp.float32)
        info = info.at[0, 0].set(valid_count[0].astype(jnp.float32))
        info = info.at[0, 1].set(assignment[0].astype(jnp.float32))
        packet_a = jnp.concatenate(
            [jnp.concatenate([key_rows[:, :cut], value_rows[:, :cut]], axis=1), info.astype(jnp.bfloat16)],
            axis=0,
        )
        packet_b = jnp.concatenate([key_rows[:, cut:], value_rows[:, cut:]], axis=1)
        got_a, got_b, ids_a, ids_b = gather_ring(packet_a, packet_b, me)
        extra = jnp.stack([g[rows_dev, :2] for g in got_a]).astype(jnp.float32).astype(jnp.int32)
        counts_of, blocks_of = extra[:, 0], extra[:, 1]
        limit_a = jnp.sum(
            jnp.where(blocks_of[:, None] == ids_a[None, :], counts_of[None, :], 0), axis=1
        )
        limit_b = jnp.sum(jnp.where(ids_b[:, None] == ids_a[None, :], limit_a[None, :], 0), axis=1)
        within = jnp.arange(rows_dev, dtype=jnp.int32)

        def half(got, limits, lo, hi):
            width = (hi - lo) * HEAD
            stack = jnp.concatenate([g[:rows_dev] for g in got], axis=0)
            keys = stack[:, :width].reshape(-1, hi - lo, HEAD)
            values = stack[:, width:].reshape(-1, hi - lo, HEAD)
            keeping = (within[None, :] < limits[:, None]).reshape(-1)
            q3 = queries[:, lo * HEAD : hi * HEAD].reshape(rows_dev, hi - lo, HEAD)
            return attend_all(q3, keys, values, keeping, scale_factor)

        attention = jnp.concatenate(
            [half(got_a, limit_a, 0, heads_a), half(got_b, limit_b, heads_a, heads_here)], axis=1
        )
        partial = jnp.dot(attention, out_weight, preferred_element_type=jnp.float32)
        rows_out = hidden.shape[0]
        side = lax.axis_index("tp")
        n_tp = rows_dev // rows_out
        pieces = partial.reshape(n_tp, rows_out, partial.shape[1])
        own = jnp.take(pieces, side, axis=0)
        other = jnp.take(pieces, 1 - side, axis=0).astype(jnp.bfloat16)
        came = lax.ppermute(other, "tp", [(0, 1), (1, 0)])
        summed = own + came.astype(jnp.float32)
        return (hidden.astype(jnp.float32) + gate_scale * summed).astype(jnp.bfloat16)

    placed = (
        P(("seq", "tp"), None),
        P("seq", "tp"),
        P("seq", "tp"),
        P("seq", "tp"),
        P(),
        P("tp", None),
        P("seq"),
        P("seq"),
    )
    return jax.shard_map(
        on_device, mesh=mesh, in_specs=placed, out_specs=P(("seq", "tp"), None), check_vma=False
    )
```

```python
import math

import jax
import jax.numpy as jnp
from jax import lax
from jax.sharding import PartitionSpec as P

HEAD = 128
neg_large = -1e30


def snake_ring(chips):
    half = chips // 2
    return [2 * a for a in range(half)] + [2 * a + 1 for a in reversed(range(half))]


def build(n_seq):
    chips = n_seq // 2
    ring = snake_ring(chips)
    half = chips // 2
    forward = [(ring[p] * 2 + c, ring[(p + 1) % chips] * 2 + c) for p in range(chips) for c in range(2)]
    backward = [(ring[(p + 1) % chips] * 2 + c, ring[p] * 2 + c) for p in range(chips) for c in range(2)]
    swap = [(i, i ^ 1) for i in range(n_seq)]

    def chip_at(pos):
        return jnp.where(pos < half, 2 * pos, 2 * (chips - 1 - pos) + 1)

    def gather_ring(packet_a, packet_b, me):
        chip = me // 2
        core = me % 2
        pos = jnp.where(chip % 2 == 0, chip // 2, chips - 1 - chip // 2)
        got_a, got_b, ids_a, ids_b = [], [], [], []
        cur_a, cur_b = packet_a, packet_b
        for step in range(chips):
            if step > 0:
                cur_a = lax.ppermute(cur_a, "seq", forward)
                cur_b = lax.ppermute(cur_b, "seq", backward)
            src_a = chip_at((pos - step) % chips) * 2 + core
            src_b = chip_at((pos + step) % chips) * 2 + core
            mate_a = lax.ppermute(cur_a, "seq", swap)
            mate_b = lax.ppermute(cur_b, "seq", swap)
            got_a += [cur_a, mate_a]
            got_b += [cur_b, mate_b]
            ids_a += [src_a, src_a ^ 1]
            ids_b += [src_b, src_b ^ 1]
        return got_a, got_b, jnp.stack(ids_a), jnp.stack(ids_b)

    return gather_ring


def attend_part(queries_3d, keys, values, keeping, scale_factor):
    scores = (
        jnp.einsum("qhd,khd->hqk", queries_3d, keys, preferred_element_type=jnp.float32)
        * scale_factor
    )
    masked = jnp.where(keeping[None, None, :], scores, neg_large)
    peak = jnp.max(masked, axis=2, keepdims=True)
    weights = jnp.where(keeping[None, None, :], jnp.exp(masked - peak), 0.0)
    totals = jnp.sum(weights, axis=2, keepdims=True)
    summed = jnp.einsum(
        "hqk,khd->hqd", weights.astype(jnp.bfloat16), values, preferred_element_type=jnp.float32
    )
    return peak, totals, summed


def combine(parts, rows_dev):
    peak = parts[0][0]
    for part in parts[1:]:
        peak = jnp.maximum(peak, part[0])
    totals = 0.0
    summed = 0.0
    for part_peak, part_totals, part_summed in parts:
        factor = jnp.exp(part_peak - peak)
        totals = totals + factor * part_totals
        summed = summed + factor * part_summed
    result = (summed / totals).astype(jnp.bfloat16)
    return result.transpose(1, 0, 2).reshape(rows_dev, -1)


def solution(mesh):
    n_seq = mesh.shape["seq"]
    gather_ring = build(n_seq)

    def on_device(
        hidden, queries, key_rows, value_rows, gate_scale, out_weight, valid_count, assignment
    ):
        rows_dev = queries.shape[0]
        heads_here = queries.shape[1] // HEAD
        heads_a = heads_here // 2
        cut = heads_a * HEAD
        scale_factor = 1.0 / math.sqrt(HEAD)
        me = lax.axis_index("seq")
        info = jnp.zeros((1, 2 * cut), jnp.float32)
        info = info.at[0, 0].set(valid_count[0].astype(jnp.float32))
        info = info.at[0, 1].set(assignment[0].astype(jnp.float32))
        info = info.astype(jnp.bfloat16)
        packet_a = jnp.concatenate(
            [jnp.concatenate([key_rows[:, :cut], value_rows[:, :cut]], axis=1), info], axis=0
        )
        packet_b = jnp.concatenate(
            [jnp.concatenate([key_rows[:, cut:], value_rows[:, cut:]], axis=1), info], axis=0
        )
        got_a, got_b, ids_a, ids_b = gather_ring(packet_a, packet_b, me)
        chips = n_seq // 2
        known = chips // 2
        seen = 2 * (known + 1)
        heard = got_a[:seen] + got_b[:seen]
        heard_ids = jnp.concatenate([ids_a[:seen], ids_b[:seen]])
        extra = jnp.stack([g[rows_dev, :2] for g in heard]).astype(jnp.float32).astype(jnp.int32)
        counts_of, blocks_of = extra[:, 0], extra[:, 1]

        def limits_for(ids):
            clip = jnp.max(jnp.where(ids[:, None] == heard_ids[None, :], blocks_of[None, :], -1), axis=1)
            return jnp.max(jnp.where(clip[:, None] == heard_ids[None, :], counts_of[None, :], -1), axis=1)

        limit_a = limits_for(ids_a)
        limit_b = limits_for(ids_b)
        within = jnp.arange(rows_dev, dtype=jnp.int32)
        phases = [(0, known + 1), (known + 1, chips - 1), (chips - 1, chips)]
        phases = [(2 * lo, 2 * hi) for lo, hi in phases if hi > lo]

        def half(got, limits, lo, hi):
            width = (hi - lo) * HEAD
            q3 = queries[:, lo * HEAD : hi * HEAD].reshape(rows_dev, hi - lo, HEAD)
            parts = []
            for first, last in phases:
                stack = jnp.concatenate([g[:rows_dev] for g in got[first:last]], axis=0)
                keys = stack[:, :width].reshape(-1, hi - lo, HEAD)
                values = stack[:, width:].reshape(-1, hi - lo, HEAD)
                keeping = (within[None, :] < limits[first:last, None]).reshape(-1)
                parts.append(attend_part(q3, keys, values, keeping, scale_factor))
            return combine(parts, rows_dev)

        attention = jnp.concatenate(
            [half(got_a, limit_a, 0, heads_a), half(got_b, limit_b, heads_a, heads_here)], axis=1
        )
        partial = jnp.dot(attention, out_weight, preferred_element_type=jnp.float32)
        rows_out = hidden.shape[0]
        side = lax.axis_index("tp")
        n_tp = rows_dev // rows_out
        pieces = partial.reshape(n_tp, rows_out, partial.shape[1])
        own = jnp.take(pieces, side, axis=0)
        other = jnp.take(pieces, 1 - side, axis=0).astype(jnp.bfloat16)
        came = lax.ppermute(other, "tp", [(0, 1), (1, 0)])
        summed = own + came.astype(jnp.float32)
        return (hidden.astype(jnp.float32) + gate_scale * summed).astype(jnp.bfloat16)

    placed = (
        P(("seq", "tp"), None),
        P("seq", "tp"),
        P("seq", "tp"),
        P("seq", "tp"),
        P(),
        P("tp", None),
        P("seq"),
        P("seq"),
    )
    return jax.shard_map(
        on_device, mesh=mesh, in_specs=placed, out_specs=P(("seq", "tp"), None), check_vma=False
    )
```

```python
import math

import jax
import jax.numpy as jnp
from jax import lax
from jax.sharding import PartitionSpec as P

HEAD = 128
neg_large = -1e30


def snake_ring(chips):
    half = chips // 2
    return [2 * a for a in range(half)] + [2 * a + 1 for a in reversed(range(half))]


def build(n_seq):
    chips = n_seq // 2
    ring = snake_ring(chips)
    half = chips // 2
    forward = [(ring[p] * 2 + c, ring[(p + 1) % chips] * 2 + c) for p in range(chips) for c in range(2)]
    backward = [(ring[(p + 1) % chips] * 2 + c, ring[p] * 2 + c) for p in range(chips) for c in range(2)]
    swap = [(i, i ^ 1) for i in range(n_seq)]

    def chip_at(pos):
        return jnp.where(pos < half, 2 * pos, 2 * (chips - 1 - pos) + 1)

    def gather_ring(packet_a, packet_b, me):
        chip = me // 2
        core = me % 2
        pos = jnp.where(chip % 2 == 0, chip // 2, chips - 1 - chip // 2)
        got_a, got_b, ids_a, ids_b = [], [], [], []
        cur_a, cur_b = packet_a, packet_b
        for step in range(chips):
            if step > 0:
                cur_a = lax.ppermute(cur_a, "seq", forward)
                cur_b = lax.ppermute(cur_b, "seq", backward)
            src_a = chip_at((pos - step) % chips) * 2 + core
            src_b = chip_at((pos + step) % chips) * 2 + core
            mate_a = lax.ppermute(cur_a, "seq", swap)
            mate_b = lax.ppermute(cur_b, "seq", swap)
            got_a += [cur_a, mate_a]
            got_b += [cur_b, mate_b]
            ids_a += [src_a, src_a ^ 1]
            ids_b += [src_b, src_b ^ 1]
        return got_a, got_b, jnp.stack(ids_a), jnp.stack(ids_b)

    return gather_ring


def attend_part(queries_3d, keys, values, keeping, scale_factor):
    scores = (
        jnp.einsum("qhd,khd->hqk", queries_3d, keys, preferred_element_type=jnp.float32)
        * scale_factor
    )
    masked = jnp.where(keeping[None, None, :], scores, neg_large)
    peak = jnp.max(masked, axis=2, keepdims=True)
    weights = jnp.where(keeping[None, None, :], jnp.exp(masked - peak), 0.0)
    totals = jnp.sum(weights, axis=2, keepdims=True)
    summed = jnp.einsum(
        "hqk,khd->hqd", weights.astype(jnp.bfloat16), values, preferred_element_type=jnp.float32
    )
    return peak, totals, summed


def combine(parts, rows_dev):
    peak = parts[0][0]
    for part in parts[1:]:
        peak = jnp.maximum(peak, part[0])
    totals = 0.0
    summed = 0.0
    for part_peak, part_totals, part_summed in parts:
        factor = jnp.exp(part_peak - peak)
        totals = totals + factor * part_totals
        summed = summed + factor * part_summed
    result = (summed / totals).astype(jnp.bfloat16)
    return result.transpose(1, 0, 2).reshape(rows_dev, -1)


def solution(mesh):
    n_seq = mesh.shape["seq"]
    gather_ring = build(n_seq)

    def on_device(
        hidden, queries, key_rows, value_rows, gate_scale, out_weight, valid_count, assignment
    ):
        rows_dev = queries.shape[0]
        heads_here = queries.shape[1] // HEAD
        heads_a = heads_here // 2
        cut = heads_a * HEAD
        scale_factor = 1.0 / math.sqrt(HEAD)
        me = lax.axis_index("seq")
        rows_pad = (rows_dev + 1 + 7) // 8 * 8
        row_id = lax.broadcasted_iota(jnp.int32, (rows_pad - rows_dev, 2 * cut), 0)
        col_id = lax.broadcasted_iota(jnp.int32, (rows_pad - rows_dev, 2 * cut), 1)
        info = jnp.where(
            (row_id == 0) & (col_id == 0),
            valid_count[0],
            jnp.where((row_id == 0) & (col_id == 1), assignment[0], 0),
        ).astype(jnp.bfloat16)
        packet_a = jnp.concatenate(
            [jnp.concatenate([key_rows[:, :cut], value_rows[:, :cut]], axis=1), info], axis=0
        )
        packet_b = jnp.concatenate(
            [jnp.concatenate([key_rows[:, cut:], value_rows[:, cut:]], axis=1), info], axis=0
        )
        got_a, got_b, ids_a, ids_b = gather_ring(packet_a, packet_b, me)
        chips = n_seq // 2
        known = chips // 2
        seen = 2 * (known + 1)
        heard = got_a[:seen] + got_b[:seen]
        heard_ids = jnp.concatenate([ids_a[:seen], ids_b[:seen]])
        extra = jnp.stack([g[rows_dev, :2] for g in heard]).astype(jnp.float32).astype(jnp.int32)
        counts_of, blocks_of = extra[:, 0], extra[:, 1]

        def limits_for(ids):
            clip = jnp.max(jnp.where(ids[:, None] == heard_ids[None, :], blocks_of[None, :], -1), axis=1)
            return jnp.max(jnp.where(clip[:, None] == heard_ids[None, :], counts_of[None, :], -1), axis=1)

        limit_a = limits_for(ids_a)
        limit_b = limits_for(ids_b)
        within = jnp.arange(rows_pad, dtype=jnp.int32)
        phases = [(0, known + 1), (known + 1, chips - 1), (chips - 1, chips)]
        phases = [(2 * lo, 2 * hi) for lo, hi in phases if hi > lo]

        def half(got, limits, lo, hi):
            width = (hi - lo) * HEAD
            q3 = queries[:, lo * HEAD : hi * HEAD].reshape(rows_dev, hi - lo, HEAD)
            parts = []
            for first, last in phases:
                stack = jnp.stack(got[first:last])
                keys = stack[:, :, :width].reshape(-1, hi - lo, HEAD)
                values = stack[:, :, width:].reshape(-1, hi - lo, HEAD)
                keeping = (within[None, :] < limits[first:last, None]).reshape(-1)
                parts.append(attend_part(q3, keys, values, keeping, scale_factor))
            return combine(parts, rows_dev)

        attention = jnp.concatenate(
            [half(got_a, limit_a, 0, heads_a), half(got_b, limit_b, heads_a, heads_here)], axis=1
        )
        partial = jnp.dot(attention, out_weight, preferred_element_type=jnp.float32)
        rows_out = hidden.shape[0]
        side = lax.axis_index("tp")
        n_tp = rows_dev // rows_out
        pieces = partial.reshape(n_tp, rows_out, partial.shape[1])
        own = jnp.take(pieces, side, axis=0)
        other = jnp.take(pieces, 1 - side, axis=0).astype(jnp.bfloat16)
        came = lax.ppermute(other, "tp", [(0, 1), (1, 0)])
        summed = own + came.astype(jnp.float32)
        return (hidden.astype(jnp.float32) + gate_scale * summed).astype(jnp.bfloat16)

    placed = (
        P(("seq", "tp"), None),
        P("seq", "tp"),
        P("seq", "tp"),
        P("seq", "tp"),
        P(),
        P("tp", None),
        P("seq"),
        P("seq"),
    )
    return jax.shard_map(
        on_device, mesh=mesh, in_specs=placed, out_specs=P(("seq", "tp"), None), check_vma=False
    )
```

```python
import math

import jax
import jax.numpy as jnp
from jax import lax
from jax.sharding import PartitionSpec as P

HEAD = 128
neg_large = -1e30


def snake_ring(chips):
    half = chips // 2
    return [2 * a for a in range(half)] + [2 * a + 1 for a in reversed(range(half))]


def attend_part(queries_3d, keys, values, keeping, scale_factor):
    scores = (
        jnp.einsum("qhd,khd->hqk", queries_3d, keys, preferred_element_type=jnp.float32)
        * scale_factor
    )
    masked = jnp.where(keeping[None, None, :], scores, neg_large)
    peak = jnp.max(masked, axis=2, keepdims=True)
    weights = jnp.where(keeping[None, None, :], jnp.exp(masked - peak), 0.0)
    totals = jnp.sum(weights, axis=2, keepdims=True)
    summed = jnp.einsum(
        "hqk,khd->hqd", weights.astype(jnp.bfloat16), values, preferred_element_type=jnp.float32
    )
    return peak, totals, summed


def combine(parts, rows_dev):
    peak = parts[0][0]
    for part in parts[1:]:
        peak = jnp.maximum(peak, part[0])
    totals = 0.0
    summed = 0.0
    for part_peak, part_totals, part_summed in parts:
        factor = jnp.exp(part_peak - peak)
        totals = totals + factor * part_totals
        summed = summed + factor * part_summed
    result = (summed / totals).astype(jnp.bfloat16)
    return result.transpose(1, 0, 2).reshape(rows_dev, -1)


def solution(mesh):
    n_seq = mesh.shape["seq"]
    chips = n_seq // 2
    ring = snake_ring(chips)
    half = chips // 2
    ring_pairs = [(ring[p] * 2, ring[(p + 1) % chips] * 2) for p in range(chips)] + [
        (ring[(p + 1) % chips] * 2 + 1, ring[p] * 2 + 1) for p in range(chips)
    ]
    swap = [(i, i ^ 1) for i in range(n_seq)]

    def chip_at(pos):
        return jnp.where(pos < half, 2 * pos, 2 * (chips - 1 - pos) + 1)

    def on_device(
        hidden, queries, key_rows, value_rows, gate_scale, out_weight, valid_count, assignment
    ):
        rows_dev = queries.shape[0]
        heads_here = queries.shape[1] // HEAD
        heads_g = heads_here // 2
        cut = heads_g * HEAD
        scale_factor = 1.0 / math.sqrt(HEAD)
        me = lax.axis_index("seq")
        chip = me // 2
        core = me % 2
        first_core = core == 0
        pos = jnp.where(chip % 2 == 0, chip // 2, chips - 1 - chip // 2)
        step_dir = 1 - 2 * core

        rows_pad = (rows_dev + 1 + 7) // 8 * 8
        row_id = lax.broadcasted_iota(jnp.int32, (rows_pad - rows_dev, 2 * cut), 0)
        col_id = lax.broadcasted_iota(jnp.int32, (rows_pad - rows_dev, 2 * cut), 1)
        info = jnp.where(
            (row_id == 0) & (col_id == 0),
            valid_count[0],
            jnp.where((row_id == 0) & (col_id == 1), assignment[0], 0),
        ).astype(jnp.bfloat16)
        block_a = jnp.concatenate(
            [jnp.concatenate([key_rows[:, :cut], value_rows[:, :cut]], axis=1), info], axis=0
        )
        block_b = jnp.concatenate(
            [jnp.concatenate([key_rows[:, cut:], value_rows[:, cut:]], axis=1), info], axis=0
        )
        kept_here = jnp.where(first_core, block_a, block_b)
        given = jnp.where(first_core, block_b, block_a)
        from_mate = lax.ppermute(given, "seq", swap)
        packet = jnp.concatenate(
            [jnp.where(first_core, kept_here, from_mate), jnp.where(first_core, from_mate, kept_here)],
            axis=0,
        )

        ring_got, mate_got, ring_src, mate_src = [], [], [], []
        cur = packet
        for step in range(chips):
            if step > 0:
                cur = lax.ppermute(cur, "seq", ring_pairs)
            ring_got.append(cur)
            mate_got.append(lax.ppermute(cur, "seq", swap))
            ring_src.append(chip_at((pos - step * step_dir) % chips))
            mate_src.append(chip_at((pos + step * step_dir) % chips))
        ring_src = jnp.stack(ring_src)
        mate_src = jnp.stack(mate_src)

        known = chips // 2
        heard = ring_got[: known + 1] + mate_got[: known + 1]
        heard_chips = jnp.concatenate([ring_src[: known + 1], mate_src[: known + 1]])
        heard_ids = jnp.concatenate([heard_chips * 2, heard_chips * 2 + 1])
        extra = jnp.concatenate(
            [jnp.stack([g[rows_dev, :2] for g in heard]), jnp.stack([g[rows_pad + rows_dev, :2] for g in heard])]
        )
        extra = extra.astype(jnp.float32).astype(jnp.int32)
        counts_of, blocks_of = extra[:, 0], extra[:, 1]

        def limits_for(src):
            ids = jnp.stack([src * 2, src * 2 + 1], axis=1).reshape(-1)
            clip = jnp.max(jnp.where(ids[:, None] == heard_ids[None, :], blocks_of[None, :], -1), axis=1)
            found = jnp.max(jnp.where(clip[:, None] == heard_ids[None, :], counts_of[None, :], -1), axis=1)
            return found.reshape(-1, 2)

        limit_ring = limits_for(ring_src)
        limit_mate = limits_for(mate_src)
        within = jnp.arange(2 * rows_pad, dtype=jnp.int32)
        local = within % rows_pad
        which = within // rows_pad
        phases = [(0, known + 1), (known + 1, chips - 1), (chips - 1, chips)]
        phases = [(lo, hi) for lo, hi in phases if hi > lo]
        q_a = queries[:, :cut].reshape(rows_dev, heads_g, HEAD)
        q_b = queries[:, cut:].reshape(rows_dev, heads_g, HEAD)
        q_ring = jnp.where(first_core, q_a, q_b)
        q_mate = jnp.where(first_core, q_b, q_a)

        def group(got, limits, q3):
            parts = []
            for lo, hi in phases:
                stack = jnp.concatenate(got[lo:hi], axis=0)
                keys = stack[:, :cut].reshape(-1, heads_g, HEAD)
                values = stack[:, cut:].reshape(-1, heads_g, HEAD)
                bound = jnp.take_along_axis(limits[lo:hi], jnp.broadcast_to(which[None, :], (hi - lo, 2 * rows_pad)), axis=1)
                keeping = (local[None, :] < bound).reshape(-1)
                parts.append(attend_part(q3, keys, values, keeping, scale_factor))
            return combine(parts, rows_dev)

        out_ring = group(ring_got, limit_ring, q_ring)
        out_mate = group(mate_got, limit_mate, q_mate)
        attention = jnp.concatenate(
            [jnp.where(first_core, out_ring, out_mate), jnp.where(first_core, out_mate, out_ring)], axis=1
        )
        partial = jnp.dot(attention, out_weight, preferred_element_type=jnp.float32)
        rows_out = hidden.shape[0]
        side = lax.axis_index("tp")
        n_tp = rows_dev // rows_out
        pieces = partial.reshape(n_tp, rows_out, partial.shape[1])
        own = jnp.take(pieces, side, axis=0)
        other = jnp.take(pieces, 1 - side, axis=0).astype(jnp.bfloat16)
        came = lax.ppermute(other, "tp", [(0, 1), (1, 0)])
        summed = own + came.astype(jnp.float32)
        return (hidden.astype(jnp.float32) + gate_scale * summed).astype(jnp.bfloat16)

    placed = (
        P(("seq", "tp"), None),
        P("seq", "tp"),
        P("seq", "tp"),
        P("seq", "tp"),
        P(),
        P("tp", None),
        P("seq"),
        P("seq"),
    )
    return jax.shard_map(
        on_device, mesh=mesh, in_specs=placed, out_specs=P(("seq", "tp"), None), check_vma=False
    )
```

```python
import math

import jax
import jax.numpy as jnp
from jax import lax
from jax.sharding import PartitionSpec as P

HEAD = 128
neg_large = -1e30


def snake_ring(chips):
    half = chips // 2
    return [2 * a for a in range(half)] + [2 * a + 1 for a in reversed(range(half))]


def build(n_seq):
    chips = n_seq // 2
    ring = snake_ring(chips)
    half = chips // 2
    forward = [(ring[p] * 2 + c, ring[(p + 1) % chips] * 2 + c) for p in range(chips) for c in range(2)]
    backward = [(ring[(p + 1) % chips] * 2 + c, ring[p] * 2 + c) for p in range(chips) for c in range(2)]
    swap = [(i, i ^ 1) for i in range(n_seq)]

    def chip_at(pos):
        return jnp.where(pos < half, 2 * pos, 2 * (chips - 1 - pos) + 1)

    def gather_ring(packet_a, packet_b, me):
        chip = me // 2
        core = me % 2
        pos = jnp.where(chip % 2 == 0, chip // 2, chips - 1 - chip // 2)
        got_a, got_b, ids_a, ids_b = [], [], [], []
        cur_a, cur_b = packet_a, packet_b
        for step in range(chips):
            if step > 0:
                cur_a = lax.ppermute(cur_a, "seq", forward)
                cur_b = lax.ppermute(cur_b, "seq", backward)
            src_a = chip_at((pos - step) % chips) * 2 + core
            src_b = chip_at((pos + step) % chips) * 2 + core
            mate_a = lax.ppermute(cur_a, "seq", swap)
            mate_b = lax.ppermute(cur_b, "seq", swap)
            got_a += [cur_a, mate_a]
            got_b += [cur_b, mate_b]
            ids_a += [src_a, src_a ^ 1]
            ids_b += [src_b, src_b ^ 1]
        return got_a, got_b, jnp.stack(ids_a), jnp.stack(ids_b)

    return gather_ring


def attend_part(queries_3d, keys, values, keeping, scale_factor):
    scores = (
        jnp.einsum("qhd,khd->hqk", queries_3d, keys, preferred_element_type=jnp.float32)
        * scale_factor
    )
    masked = jnp.where(keeping[None, None, :], scores, neg_large)
    peak = jnp.max(masked, axis=2, keepdims=True)
    weights = jnp.where(keeping[None, None, :], jnp.exp(masked - peak), 0.0)
    totals = jnp.sum(weights, axis=2, keepdims=True)
    summed = jnp.einsum(
        "hqk,khd->hqd", weights.astype(jnp.bfloat16), values, preferred_element_type=jnp.float32
    )
    return peak, totals, summed


def combine(parts, rows_dev):
    peak = parts[0][0]
    for part in parts[1:]:
        peak = jnp.maximum(peak, part[0])
    totals = 0.0
    summed = 0.0
    for part_peak, part_totals, part_summed in parts:
        factor = jnp.exp(part_peak - peak)
        totals = totals + factor * part_totals
        summed = summed + factor * part_summed
    result = (summed / totals).astype(jnp.bfloat16)
    return result.transpose(1, 0, 2).reshape(rows_dev, -1)


def solution(mesh):
    n_seq = mesh.shape["seq"]
    gather_ring = build(n_seq)

    def on_device(
        hidden, queries, key_rows, value_rows, gate_scale, out_weight, valid_count, assignment
    ):
        rows_dev = queries.shape[0]
        heads_here = queries.shape[1] // HEAD
        heads_a = heads_here // 2
        cut = heads_a * HEAD
        scale_factor = 1.0 / math.sqrt(HEAD)
        me = lax.axis_index("seq")
        rows_pad = (rows_dev + 1 + 7) // 8 * 8
        row_id = lax.broadcasted_iota(jnp.int32, (rows_pad - rows_dev, 2 * cut), 0)
        col_id = lax.broadcasted_iota(jnp.int32, (rows_pad - rows_dev, 2 * cut), 1)
        info = jnp.where(
            (row_id == 0) & (col_id == 0),
            valid_count[0],
            jnp.where((row_id == 0) & (col_id == 1), assignment[0], 0),
        ).astype(jnp.bfloat16)
        packet_a = jnp.concatenate(
            [jnp.concatenate([key_rows[:, :cut], value_rows[:, :cut]], axis=1), info], axis=0
        )
        packet_b = jnp.concatenate(
            [jnp.concatenate([key_rows[:, cut:], value_rows[:, cut:]], axis=1), info], axis=0
        )
        got_a, got_b, ids_a, ids_b = gather_ring(packet_a, packet_b, me)
        chips = n_seq // 2
        known = chips // 2
        seen = 2 * (known + 1)
        heard = got_a[:seen] + got_b[:seen]
        heard_ids = jnp.concatenate([ids_a[:seen], ids_b[:seen]])
        extra = jnp.stack([g[rows_dev, :2] for g in heard]).astype(jnp.float32).astype(jnp.int32)
        counts_of, blocks_of = extra[:, 0], extra[:, 1]

        def limits_for(ids):
            clip = jnp.max(jnp.where(ids[:, None] == heard_ids[None, :], blocks_of[None, :], -1), axis=1)
            return jnp.max(jnp.where(clip[:, None] == heard_ids[None, :], counts_of[None, :], -1), axis=1)

        limit_a = limits_for(ids_a)
        limit_b = limits_for(ids_b)
        within = jnp.arange(rows_pad, dtype=jnp.int32)
        phases = [(0, known + 1), (known + 1, chips - 1), (chips - 1, chips)]
        phases = [(2 * lo, 2 * hi) for lo, hi in phases if hi > lo]

        def half(got, limits, lo, hi):
            width = (hi - lo) * HEAD
            q3 = queries[:, lo * HEAD : hi * HEAD].reshape(rows_dev, hi - lo, HEAD)
            parts = []
            for first, last in phases:
                stack = jnp.concatenate(got[first:last], axis=0)
                keys = stack[:, :width].reshape(-1, hi - lo, HEAD)
                values = stack[:, width:].reshape(-1, hi - lo, HEAD)
                keeping = (within[None, :] < limits[first:last, None]).reshape(-1)
                parts.append(attend_part(q3, keys, values, keeping, scale_factor))
            return combine(parts, rows_dev)

        attention = jnp.concatenate(
            [half(got_a, limit_a, 0, heads_a), half(got_b, limit_b, heads_a, heads_here)], axis=1
        )
        partial = jnp.dot(attention, out_weight, preferred_element_type=jnp.float32)
        rows_out = hidden.shape[0]
        side = lax.axis_index("tp")
        n_tp = rows_dev // rows_out
        pieces = partial.reshape(n_tp, rows_out, partial.shape[1])
        own = jnp.take(pieces, side, axis=0)
        other = jnp.take(pieces, 1 - side, axis=0).astype(jnp.bfloat16)
        came = lax.ppermute(other, "tp", [(0, 1), (1, 0)])
        summed = own + came.astype(jnp.float32)
        return (hidden.astype(jnp.float32) + gate_scale * summed).astype(jnp.bfloat16)

    placed = (
        P(("seq", "tp"), None),
        P("seq", "tp"),
        P("seq", "tp"),
        P("seq", "tp"),
        P(),
        P("tp", None),
        P("seq"),
        P("seq"),
    )
    return jax.shard_map(
        on_device, mesh=mesh, in_specs=placed, out_specs=P(("seq", "tp"), None), check_vma=False
    )
```

```python
import math

import jax
import jax.numpy as jnp
from jax import lax
from jax.sharding import PartitionSpec as P

HEAD = 128
neg_large = -1e30


def snake_ring(chips):
    half = chips // 2
    return [2 * a for a in range(half)] + [2 * a + 1 for a in reversed(range(half))]


def build(n_seq):
    chips = n_seq // 2
    ring = snake_ring(chips)
    half = chips // 2
    forward = [(ring[p] * 2 + c, ring[(p + 1) % chips] * 2 + c) for p in range(chips) for c in range(2)]
    backward = [(ring[(p + 1) % chips] * 2 + c, ring[p] * 2 + c) for p in range(chips) for c in range(2)]
    swap = [(i, i ^ 1) for i in range(n_seq)]

    def chip_at(pos):
        return jnp.where(pos < half, 2 * pos, 2 * (chips - 1 - pos) + 1)

    def gather_ring(packet_a, packet_b, me):
        chip = me // 2
        core = me % 2
        pos = jnp.where(chip % 2 == 0, chip // 2, chips - 1 - chip // 2)
        got_a, got_b, ids_a, ids_b = [], [], [], []
        cur_a, cur_b = packet_a, packet_b
        for step in range(chips):
            if step > 0:
                cur_a = lax.ppermute(cur_a, "seq", forward)
                cur_b = lax.ppermute(cur_b, "seq", backward)
            src_a = chip_at((pos - step) % chips) * 2 + core
            src_b = chip_at((pos + step) % chips) * 2 + core
            mate_a = lax.ppermute(cur_a, "seq", swap)
            mate_b = lax.ppermute(cur_b, "seq", swap)
            got_a += [cur_a, mate_a]
            got_b += [cur_b, mate_b]
            ids_a += [src_a, src_a ^ 1]
            ids_b += [src_b, src_b ^ 1]
        return got_a, got_b, jnp.stack(ids_a), jnp.stack(ids_b)

    return gather_ring


def attend_part(queries_3d, keys, values, keeping, scale_factor):
    scores = (
        jnp.einsum("qhd,khd->hqk", queries_3d, keys, preferred_element_type=jnp.float32)
        * scale_factor
    )
    masked = jnp.where(keeping[None, None, :], scores, neg_large)
    peak = jnp.max(masked, axis=2, keepdims=True)
    weights = jnp.where(keeping[None, None, :], jnp.exp(masked - peak), 0.0)
    totals = jnp.sum(weights, axis=2, keepdims=True)
    summed = jnp.einsum(
        "hqk,khd->hqd", weights.astype(jnp.bfloat16), values, preferred_element_type=jnp.float32
    )
    return peak, totals, summed


def combine(parts, rows_dev):
    peak = parts[0][0]
    for part in parts[1:]:
        peak = jnp.maximum(peak, part[0])
    totals = 0.0
    summed = 0.0
    for part_peak, part_totals, part_summed in parts:
        factor = jnp.exp(part_peak - peak)
        totals = totals + factor * part_totals
        summed = summed + factor * part_summed
    result = (summed / totals).astype(jnp.bfloat16)
    return result.transpose(1, 0, 2).reshape(rows_dev, -1)


def solution(mesh):
    n_seq = mesh.shape["seq"]
    gather_ring = build(n_seq)

    def on_device(
        hidden, queries, key_rows, value_rows, gate_scale, out_weight, valid_count, assignment
    ):
        rows_dev = queries.shape[0]
        heads_here = queries.shape[1] // HEAD
        heads_a = heads_here // 2
        cut = heads_a * HEAD
        scale_factor = 1.0 / math.sqrt(HEAD)
        me = lax.axis_index("seq")
        rows_pad = (rows_dev + 1 + 7) // 8 * 8
        row_id = lax.broadcasted_iota(jnp.int32, (rows_pad - rows_dev, 2 * cut), 0)
        col_id = lax.broadcasted_iota(jnp.int32, (rows_pad - rows_dev, 2 * cut), 1)
        info = jnp.where(
            (row_id == 0) & (col_id == 0),
            valid_count[0],
            jnp.where((row_id == 0) & (col_id == 1), assignment[0], 0),
        ).astype(jnp.bfloat16)
        packet_a = jnp.concatenate(
            [jnp.concatenate([key_rows[:, :cut], value_rows[:, :cut]], axis=1), info], axis=0
        )
        packet_b = jnp.concatenate(
            [jnp.concatenate([key_rows[:, cut:], value_rows[:, cut:]], axis=1), info], axis=0
        )
        got_a, got_b, ids_a, ids_b = gather_ring(packet_a, packet_b, me)
        chips = n_seq // 2
        known = chips // 2
        seen = 2 * (known + 1)
        heard = got_a[:seen] + got_b[:seen]
        heard_ids = jnp.concatenate([ids_a[:seen], ids_b[:seen]])
        extra = jnp.stack([g[rows_dev, :2] for g in heard]).astype(jnp.float32).astype(jnp.int32)
        counts_of, blocks_of = extra[:, 0], extra[:, 1]

        def limits_for(ids):
            clip = jnp.max(jnp.where(ids[:, None] == heard_ids[None, :], blocks_of[None, :], -1), axis=1)
            return jnp.max(jnp.where(clip[:, None] == heard_ids[None, :], counts_of[None, :], -1), axis=1)

        limit_a = limits_for(ids_a)
        limit_b = limits_for(ids_b)
        within = jnp.arange(rows_pad, dtype=jnp.int32)
        phases = [(0, known + 1), (known + 1, chips - 1), (chips - 1, chips)]
        phases = [(2 * lo, 2 * hi) for lo, hi in phases if hi > lo]

        def half(got, limits, lo, hi):
            width = (hi - lo) * HEAD
            q3 = queries[:, lo * HEAD : hi * HEAD].reshape(rows_dev, hi - lo, HEAD)
            parts = []
            for first, last in phases:
                stack = jnp.concatenate(got[first:last], axis=0)
                keys = stack[:, :width].reshape(-1, hi - lo, HEAD)
                values = stack[:, width:].reshape(-1, hi - lo, HEAD)
                keeping = (within[None, :] < limits[first:last, None]).reshape(-1)
                parts.append(attend_part(q3, keys, values, keeping, scale_factor))
            return combine(parts, rows_dev)

        attention = jnp.concatenate(
            [half(got_a, limit_a, 0, heads_a), half(got_b, limit_b, heads_a, heads_here)], axis=1
        )
        rows_out = hidden.shape[0]
        side = lax.axis_index("tp")
        n_tp = rows_dev // rows_out
        width_all = out_weight.shape[1]
        n_chunks = 4 if width_all % (4 * HEAD) == 0 else 1
        width = width_all // n_chunks
        mixed = []
        for i in range(n_chunks):
            cols = slice(i * width, (i + 1) * width)
            partial = jnp.dot(attention, out_weight[:, cols], preferred_element_type=jnp.float32)
            pieces = partial.reshape(n_tp, rows_out, width)
            own = jnp.take(pieces, side, axis=0)
            other = jnp.take(pieces, 1 - side, axis=0).astype(jnp.bfloat16)
            came = lax.ppermute(other, "tp", [(0, 1), (1, 0)])
            summed = own + came.astype(jnp.float32)
            mixed.append(
                (hidden[:, cols].astype(jnp.float32) + gate_scale[cols] * summed).astype(jnp.bfloat16)
            )
        return jnp.concatenate(mixed, axis=1)

    placed = (
        P(("seq", "tp"), None),
        P("seq", "tp"),
        P("seq", "tp"),
        P("seq", "tp"),
        P(),
        P("tp", None),
        P("seq"),
        P("seq"),
    )
    return jax.shard_map(
        on_device, mesh=mesh, in_specs=placed, out_specs=P(("seq", "tp"), None), check_vma=False
    )
```

```python
import math

import jax
import jax.numpy as jnp
from jax import lax
from jax.sharding import PartitionSpec as P

HEAD = 128
neg_large = -1e30


def snake_ring(chips):
    half = chips // 2
    return [2 * a for a in range(half)] + [2 * a + 1 for a in reversed(range(half))]


def build(n_seq):
    chips = n_seq // 2
    ring = snake_ring(chips)
    half = chips // 2
    forward = [(ring[p] * 2 + c, ring[(p + 1) % chips] * 2 + c) for p in range(chips) for c in range(2)]
    backward = [(ring[(p + 1) % chips] * 2 + c, ring[p] * 2 + c) for p in range(chips) for c in range(2)]
    swap = [(i, i ^ 1) for i in range(n_seq)]

    def chip_at(pos):
        return jnp.where(pos < half, 2 * pos, 2 * (chips - 1 - pos) + 1)

    def gather_ring(packet_a, packet_b, me):
        chip = me // 2
        core = me % 2
        pos = jnp.where(chip % 2 == 0, chip // 2, chips - 1 - chip // 2)
        got_a, got_b, ids_a, ids_b = [], [], [], []
        cur_a, cur_b = packet_a, packet_b
        for step in range(chips):
            if step > 0:
                cur_a = lax.ppermute(cur_a, "seq", forward)
                cur_b = lax.ppermute(cur_b, "seq", backward)
            src_a = chip_at((pos - step) % chips) * 2 + core
            src_b = chip_at((pos + step) % chips) * 2 + core
            mate_a = lax.ppermute(cur_a, "seq", swap)
            mate_b = lax.ppermute(cur_b, "seq", swap)
            got_a += [cur_a, mate_a]
            got_b += [cur_b, mate_b]
            ids_a += [src_a, src_a ^ 1]
            ids_b += [src_b, src_b ^ 1]
        return got_a, got_b, jnp.stack(ids_a), jnp.stack(ids_b)

    return gather_ring


def attend_part(queries_3d, keys, values, keeping, scale_factor):
    scores = (
        jnp.einsum("qhd,khd->hqk", queries_3d, keys, preferred_element_type=jnp.float32)
        * scale_factor
    )
    masked = jnp.where(keeping[None, None, :], scores, neg_large)
    peak = jnp.max(masked, axis=2, keepdims=True)
    weights = jnp.where(keeping[None, None, :], jnp.exp(masked - peak), 0.0)
    totals = jnp.sum(weights, axis=2, keepdims=True)
    summed = jnp.einsum(
        "hqk,khd->hqd", weights.astype(jnp.bfloat16), values, preferred_element_type=jnp.float32
    )
    return peak, totals, summed


def combine(parts, rows_dev):
    peak = parts[0][0]
    for part in parts[1:]:
        peak = jnp.maximum(peak, part[0])
    totals = 0.0
    summed = 0.0
    for part_peak, part_totals, part_summed in parts:
        factor = jnp.exp(part_peak - peak)
        totals = totals + factor * part_totals
        summed = summed + factor * part_summed
    result = (summed / totals).astype(jnp.bfloat16)
    return result.transpose(1, 0, 2).reshape(rows_dev, -1)


def solution(mesh):
    n_seq = mesh.shape["seq"]
    gather_ring = build(n_seq)

    def on_device(
        hidden, queries, key_rows, value_rows, gate_scale, out_weight, valid_count, assignment
    ):
        rows_dev = queries.shape[0]
        heads_here = queries.shape[1] // HEAD
        heads_a = heads_here // 2
        cut = heads_a * HEAD
        scale_factor = 1.0 / math.sqrt(HEAD)
        me = lax.axis_index("seq")
        rows_pad = (rows_dev + 1 + 7) // 8 * 8
        row_id = lax.broadcasted_iota(jnp.int32, (rows_pad - rows_dev, 2 * cut), 0)
        col_id = lax.broadcasted_iota(jnp.int32, (rows_pad - rows_dev, 2 * cut), 1)
        info = jnp.where(
            (row_id == 0) & (col_id == 0),
            valid_count[0],
            jnp.where((row_id == 0) & (col_id == 1), assignment[0], 0),
        ).astype(jnp.bfloat16)
        packet_a = jnp.concatenate(
            [jnp.concatenate([key_rows[:, :cut], value_rows[:, :cut]], axis=1), info], axis=0
        )
        packet_b = jnp.concatenate(
            [jnp.concatenate([key_rows[:, cut:], value_rows[:, cut:]], axis=1), info], axis=0
        )
        got_a, got_b, ids_a, ids_b = gather_ring(packet_a, packet_b, me)
        chips = n_seq // 2
        known = chips // 2
        seen = 2 * (known + 1)
        heard = got_a[:seen] + got_b[:seen]
        heard_ids = jnp.concatenate([ids_a[:seen], ids_b[:seen]])
        extra = jnp.stack([g[rows_dev, :2] for g in heard]).astype(jnp.float32).astype(jnp.int32)
        counts_of, blocks_of = extra[:, 0], extra[:, 1]

        def limits_for(ids):
            clip = jnp.max(jnp.where(ids[:, None] == heard_ids[None, :], blocks_of[None, :], -1), axis=1)
            return jnp.max(jnp.where(clip[:, None] == heard_ids[None, :], counts_of[None, :], -1), axis=1)

        limit_a = limits_for(ids_a)
        limit_b = limits_for(ids_b)
        within = jnp.arange(rows_pad, dtype=jnp.int32)
        phases = [(0, known + 1), (known + 1, chips - 1), (chips - 1, chips)]
        phases = [(2 * lo, 2 * hi) for lo, hi in phases if hi > lo]

        anchor = 2 * max(chips - 2, 0)
        early = 2 * (chips - 1)
        held_a, held_b, _ = lax.optimization_barrier(
            (got_a[:early], got_b[:early], (got_a[anchor], got_b[anchor]))
        )
        got_a = list(held_a) + got_a[early:]
        got_b = list(held_b) + got_b[early:]

        def half(got, limits, lo, hi):
            width = (hi - lo) * HEAD
            q3 = queries[:, lo * HEAD : hi * HEAD].reshape(rows_dev, hi - lo, HEAD)
            parts = []
            for first, last in phases:
                stack = jnp.concatenate(got[first:last], axis=0)
                keys = stack[:, :width].reshape(-1, hi - lo, HEAD)
                values = stack[:, width:].reshape(-1, hi - lo, HEAD)
                keeping = (within[None, :] < limits[first:last, None]).reshape(-1)
                parts.append(attend_part(q3, keys, values, keeping, scale_factor))
            return combine(parts, rows_dev)

        attention = jnp.concatenate(
            [half(got_a, limit_a, 0, heads_a), half(got_b, limit_b, heads_a, heads_here)], axis=1
        )
        partial = jnp.dot(attention, out_weight, preferred_element_type=jnp.float32)
        rows_out = hidden.shape[0]
        side = lax.axis_index("tp")
        n_tp = rows_dev // rows_out
        pieces = partial.reshape(n_tp, rows_out, partial.shape[1])
        own = jnp.take(pieces, side, axis=0)
        other = jnp.take(pieces, 1 - side, axis=0).astype(jnp.bfloat16)
        came = lax.ppermute(other, "tp", [(0, 1), (1, 0)])
        summed = own + came.astype(jnp.float32)
        return (hidden.astype(jnp.float32) + gate_scale * summed).astype(jnp.bfloat16)

    placed = (
        P(("seq", "tp"), None),
        P("seq", "tp"),
        P("seq", "tp"),
        P("seq", "tp"),
        P(),
        P("tp", None),
        P("seq"),
        P("seq"),
    )
    return jax.shard_map(
        on_device, mesh=mesh, in_specs=placed, out_specs=P(("seq", "tp"), None), check_vma=False
    )
```

```python
import math

import jax
import jax.numpy as jnp
from jax import lax
from jax.sharding import PartitionSpec as P

HEAD = 128
neg_large = -1e30


def snake_ring(chips):
    half = chips // 2
    return [2 * a for a in range(half)] + [2 * a + 1 for a in reversed(range(half))]


def build(n_seq):
    chips = n_seq // 2
    ring = snake_ring(chips)
    half = chips // 2
    forward = [(ring[p] * 2 + c, ring[(p + 1) % chips] * 2 + c) for p in range(chips) for c in range(2)]
    backward = [(ring[(p + 1) % chips] * 2 + c, ring[p] * 2 + c) for p in range(chips) for c in range(2)]
    swap = [(i, i ^ 1) for i in range(n_seq)]

    def chip_at(pos):
        return jnp.where(pos < half, 2 * pos, 2 * (chips - 1 - pos) + 1)

    def gather_ring(packet_a, packet_b, me):
        chip = me // 2
        core = me % 2
        pos = jnp.where(chip % 2 == 0, chip // 2, chips - 1 - chip // 2)
        got_a, got_b, ids_a, ids_b = [], [], [], []
        cur_a, cur_b = packet_a, packet_b
        for step in range(chips):
            if step > 0:
                cur_a = lax.ppermute(cur_a, "seq", forward)
                cur_b = lax.ppermute(cur_b, "seq", backward)
            src_a = chip_at((pos - step) % chips) * 2 + core
            src_b = chip_at((pos + step) % chips) * 2 + core
            mate_a = lax.ppermute(cur_a, "seq", swap)
            mate_b = lax.ppermute(cur_b, "seq", swap)
            got_a += [cur_a, mate_a]
            got_b += [cur_b, mate_b]
            ids_a += [src_a, src_a ^ 1]
            ids_b += [src_b, src_b ^ 1]
        return got_a, got_b, jnp.stack(ids_a), jnp.stack(ids_b)

    return gather_ring


def attend_part(queries_3d, keys, values, keeping, scale_factor):
    scores = (
        jnp.einsum("hqd,hkd->hqk", queries_3d, keys, preferred_element_type=jnp.float32)
        * scale_factor
    )
    masked = jnp.where(keeping[None, None, :], scores, neg_large)
    peak = jnp.max(masked, axis=2, keepdims=True)
    weights = jnp.where(keeping[None, None, :], jnp.exp(masked - peak), 0.0)
    totals = jnp.sum(weights, axis=2, keepdims=True)
    summed = jnp.einsum(
        "hqk,hkd->hqd", weights.astype(jnp.bfloat16), values, preferred_element_type=jnp.float32
    )
    return peak, totals, summed


def combine(parts, rows_dev):
    peak = parts[0][0]
    for part in parts[1:]:
        peak = jnp.maximum(peak, part[0])
    totals = 0.0
    summed = 0.0
    for part_peak, part_totals, part_summed in parts:
        factor = jnp.exp(part_peak - peak)
        totals = totals + factor * part_totals
        summed = summed + factor * part_summed
    result = (summed / totals).astype(jnp.bfloat16)
    return result.transpose(1, 0, 2).reshape(rows_dev, -1)


def solution(mesh):
    n_seq = mesh.shape["seq"]
    gather_ring = build(n_seq)

    def on_device(
        hidden, queries, key_rows, value_rows, gate_scale, out_weight, valid_count, assignment
    ):
        rows_dev = queries.shape[0]
        heads_here = queries.shape[1] // HEAD
        heads_a = heads_here // 2
        cut = heads_a * HEAD
        scale_factor = 1.0 / math.sqrt(HEAD)
        me = lax.axis_index("seq")
        rows_pad = (rows_dev + 1 + 7) // 8 * 8
        row_id = lax.broadcasted_iota(jnp.int32, (rows_pad - rows_dev, HEAD), 0)
        col_id = lax.broadcasted_iota(jnp.int32, (rows_pad - rows_dev, HEAD), 1)
        info = jnp.where(
            (row_id == 0) & (col_id == 0),
            valid_count[0],
            jnp.where((row_id == 0) & (col_id == 1), assignment[0], 0),
        ).astype(jnp.bfloat16)

        def head_major(lo, hi):
            both = jnp.concatenate([key_rows[:, lo * HEAD : hi * HEAD], value_rows[:, lo * HEAD : hi * HEAD]], axis=1)
            both = both.reshape(rows_dev, 2 * (hi - lo), HEAD).transpose(1, 0, 2)
            pad = jnp.broadcast_to(info[None], (2 * (hi - lo),) + info.shape)
            return jnp.concatenate([both, pad], axis=1)

        packet_a = head_major(0, heads_a)
        packet_b = head_major(heads_a, heads_here)
        got_a, got_b, ids_a, ids_b = gather_ring(packet_a, packet_b, me)
        chips = n_seq // 2
        known = chips // 2
        seen = 2 * (known + 1)
        heard = got_a[:seen] + got_b[:seen]
        heard_ids = jnp.concatenate([ids_a[:seen], ids_b[:seen]])
        extra = jnp.stack([g[0, rows_dev, :2] for g in heard]).astype(jnp.float32).astype(jnp.int32)
        counts_of, blocks_of = extra[:, 0], extra[:, 1]

        def limits_for(ids):
            clip = jnp.max(jnp.where(ids[:, None] == heard_ids[None, :], blocks_of[None, :], -1), axis=1)
            return jnp.max(jnp.where(clip[:, None] == heard_ids[None, :], counts_of[None, :], -1), axis=1)

        limit_a = limits_for(ids_a)
        limit_b = limits_for(ids_b)
        within = jnp.arange(rows_pad, dtype=jnp.int32)
        phases = [(0, known + 1), (known + 1, chips - 1), (chips - 1, chips)]
        phases = [(2 * lo, 2 * hi) for lo, hi in phases if hi > lo]

        anchor = 2 * max(chips - 2, 0)
        early = 2 * (chips - 1)
        held_a, held_b, _ = lax.optimization_barrier(
            (got_a[:early], got_b[:early], (got_a[anchor], got_b[anchor]))
        )
        got_a = list(held_a) + got_a[early:]
        got_b = list(held_b) + got_b[early:]

        def half(got, limits, lo, hi):
            q3 = queries[:, lo * HEAD : hi * HEAD].reshape(rows_dev, hi - lo, HEAD).transpose(1, 0, 2)
            parts = []
            for first, last in phases:
                stack = jnp.concatenate(got[first:last], axis=1)
                keys = stack[: hi - lo]
                values = stack[hi - lo :]
                keeping = (within[None, :] < limits[first:last, None]).reshape(-1)
                parts.append(attend_part(q3, keys, values, keeping, scale_factor))
            return combine(parts, rows_dev)

        attention = jnp.concatenate(
            [half(got_a, limit_a, 0, heads_a), half(got_b, limit_b, heads_a, heads_here)], axis=1
        )
        partial = jnp.dot(attention, out_weight, preferred_element_type=jnp.float32)
        rows_out = hidden.shape[0]
        side = lax.axis_index("tp")
        n_tp = rows_dev // rows_out
        pieces = partial.reshape(n_tp, rows_out, partial.shape[1])
        own = jnp.take(pieces, side, axis=0)
        other = jnp.take(pieces, 1 - side, axis=0).astype(jnp.bfloat16)
        came = lax.ppermute(other, "tp", [(0, 1), (1, 0)])
        summed = own + came.astype(jnp.float32)
        return (hidden.astype(jnp.float32) + gate_scale * summed).astype(jnp.bfloat16)

    placed = (
        P(("seq", "tp"), None),
        P("seq", "tp"),
        P("seq", "tp"),
        P("seq", "tp"),
        P(),
        P("tp", None),
        P("seq"),
        P("seq"),
    )
    return jax.shard_map(
        on_device, mesh=mesh, in_specs=placed, out_specs=P(("seq", "tp"), None), check_vma=False
    )
```

```python
import math

import jax
import jax.numpy as jnp
from jax import lax
from jax.experimental import pallas as pl
from jax.sharding import PartitionSpec as P

HEAD = 128
neg_large = -1e30


def snake_ring(chips):
    half = chips // 2
    return [2 * a for a in range(half)] + [2 * a + 1 for a in reversed(range(half))]


def build(n_seq):
    chips = n_seq // 2
    ring = snake_ring(chips)
    half = chips // 2
    forward = [(ring[p] * 2 + c, ring[(p + 1) % chips] * 2 + c) for p in range(chips) for c in range(2)]
    backward = [(ring[(p + 1) % chips] * 2 + c, ring[p] * 2 + c) for p in range(chips) for c in range(2)]
    swap = [(i, i ^ 1) for i in range(n_seq)]

    def chip_at(pos):
        return jnp.where(pos < half, 2 * pos, 2 * (chips - 1 - pos) + 1)

    def gather_ring(packet_a, packet_b, me):
        chip = me // 2
        core = me % 2
        pos = jnp.where(chip % 2 == 0, chip // 2, chips - 1 - chip // 2)
        got_a, got_b, ids_a, ids_b = [], [], [], []
        cur_a, cur_b = packet_a, packet_b
        for step in range(chips):
            if step > 0:
                cur_a = lax.ppermute(cur_a, "seq", forward)
                cur_b = lax.ppermute(cur_b, "seq", backward)
            src_a = chip_at((pos - step) % chips) * 2 + core
            src_b = chip_at((pos + step) % chips) * 2 + core
            mate_a = lax.ppermute(cur_a, "seq", swap)
            mate_b = lax.ppermute(cur_b, "seq", swap)
            got_a += [cur_a, mate_a]
            got_b += [cur_b, mate_b]
            ids_a += [src_a, src_a ^ 1]
            ids_b += [src_b, src_b ^ 1]
        return got_a, got_b, jnp.stack(ids_a), jnp.stack(ids_b)

    return gather_ring


def attend_part(queries_3d, keys, values, keeping, scale_factor):
    scores = (
        jnp.einsum("hqd,hkd->hqk", queries_3d, keys, preferred_element_type=jnp.float32)
        * scale_factor
    )
    masked = jnp.where(keeping[None, None, :], scores, neg_large)
    peak = jnp.max(masked, axis=2, keepdims=True)
    weights = jnp.where(keeping[None, None, :], jnp.exp(masked - peak), 0.0)
    totals = jnp.sum(weights, axis=2, keepdims=True)
    summed = jnp.einsum(
        "hqk,hkd->hqd", weights.astype(jnp.bfloat16), values, preferred_element_type=jnp.float32
    )
    return peak, totals, summed


def phase_kernel(count, heads, scale_factor):
    def kernel(*refs):
        q_ref, keep_ref = refs[0], refs[1]
        packets = refs[2 : 2 + count]
        peak_ref, totals_ref, summed_ref = refs[2 + count :]
        for head in range(heads):
            q = q_ref[head]
            scores = []
            for p in range(count):
                s = lax.dot_general(
                    q, packets[p][head], (((1,), (1,)), ((), ())), preferred_element_type=jnp.float32
                )
                scores.append(jnp.where(keep_ref[p] > 0, s * scale_factor, neg_large))
            peak = jnp.max(scores[0], axis=1, keepdims=True)
            for s in scores[1:]:
                peak = jnp.maximum(peak, jnp.max(s, axis=1, keepdims=True))
            totals = jnp.zeros_like(peak)
            summed = jnp.zeros((q.shape[0], q.shape[1]), jnp.float32)
            for p in range(count):
                weights = jnp.where(keep_ref[p] > 0, jnp.exp(scores[p] - peak), 0.0)
                totals = totals + jnp.sum(weights, axis=1, keepdims=True)
                summed = summed + jnp.dot(
                    weights.astype(jnp.bfloat16), packets[p][heads + head], preferred_element_type=jnp.float32
                )
            peak_ref[head] = peak
            totals_ref[head] = totals
            summed_ref[head] = summed

    return kernel


def attend_packets(q3, packets, keep, scale_factor, interpret=False):
    heads, rows, width = q3.shape
    count = len(packets)
    out_shape = (
        jax.ShapeDtypeStruct((heads, rows, 1), jnp.float32),
        jax.ShapeDtypeStruct((heads, rows, 1), jnp.float32),
        jax.ShapeDtypeStruct((heads, rows, width), jnp.float32),
    )
    return pl.pallas_call(
        phase_kernel(count, heads, scale_factor), out_shape=out_shape, interpret=interpret
    )(q3, keep, *packets)


def combine(parts, rows_dev):
    peak = parts[0][0]
    for part in parts[1:]:
        peak = jnp.maximum(peak, part[0])
    totals = 0.0
    summed = 0.0
    for part_peak, part_totals, part_summed in parts:
        factor = jnp.exp(part_peak - peak)
        totals = totals + factor * part_totals
        summed = summed + factor * part_summed
    result = (summed / totals).astype(jnp.bfloat16)
    return result.transpose(1, 0, 2).reshape(rows_dev, -1)


def solution(mesh):
    n_seq = mesh.shape["seq"]
    gather_ring = build(n_seq)

    def on_device(
        hidden, queries, key_rows, value_rows, gate_scale, out_weight, valid_count, assignment
    ):
        rows_dev = queries.shape[0]
        heads_here = queries.shape[1] // HEAD
        heads_a = heads_here // 2
        cut = heads_a * HEAD
        scale_factor = 1.0 / math.sqrt(HEAD)
        me = lax.axis_index("seq")
        rows_pad = (rows_dev + 1 + 7) // 8 * 8
        row_id = lax.broadcasted_iota(jnp.int32, (rows_pad - rows_dev, HEAD), 0)
        col_id = lax.broadcasted_iota(jnp.int32, (rows_pad - rows_dev, HEAD), 1)
        info = jnp.where(
            (row_id == 0) & (col_id == 0),
            valid_count[0],
            jnp.where((row_id == 0) & (col_id == 1), assignment[0], 0),
        ).astype(jnp.bfloat16)

        def head_major(lo, hi):
            both = jnp.concatenate([key_rows[:, lo * HEAD : hi * HEAD], value_rows[:, lo * HEAD : hi * HEAD]], axis=1)
            both = both.reshape(rows_dev, 2 * (hi - lo), HEAD).transpose(1, 0, 2)
            pad = jnp.broadcast_to(info[None], (2 * (hi - lo),) + info.shape)
            return jnp.concatenate([both, pad], axis=1)

        packet_a = head_major(0, heads_a)
        packet_b = head_major(heads_a, heads_here)
        got_a, got_b, ids_a, ids_b = gather_ring(packet_a, packet_b, me)
        chips = n_seq // 2
        known = chips // 2
        seen = 2 * (known + 1)
        heard = got_a[:seen] + got_b[:seen]
        heard_ids = jnp.concatenate([ids_a[:seen], ids_b[:seen]])
        extra = jnp.stack([g[0, rows_dev, :2] for g in heard]).astype(jnp.float32).astype(jnp.int32)
        counts_of, blocks_of = extra[:, 0], extra[:, 1]

        def limits_for(ids):
            clip = jnp.max(jnp.where(ids[:, None] == heard_ids[None, :], blocks_of[None, :], -1), axis=1)
            return jnp.max(jnp.where(clip[:, None] == heard_ids[None, :], counts_of[None, :], -1), axis=1)

        limit_a = limits_for(ids_a)
        limit_b = limits_for(ids_b)
        within = jnp.arange(rows_pad, dtype=jnp.int32)
        phases = [(0, known + 1), (known + 1, chips - 1), (chips - 1, chips)]
        phases = [(2 * lo, 2 * hi) for lo, hi in phases if hi > lo]

        anchor = 2 * max(chips - 2, 0)
        early = 2 * (chips - 1)
        held_a, held_b, _ = lax.optimization_barrier(
            (got_a[:early], got_b[:early], (got_a[anchor], got_b[anchor]))
        )
        got_a = list(held_a) + got_a[early:]
        got_b = list(held_b) + got_b[early:]

        def half(got, limits, lo, hi):
            q3 = queries[:, lo * HEAD : hi * HEAD].reshape(rows_dev, hi - lo, HEAD).transpose(1, 0, 2)
            parts = []
            for first, last in phases:
                keep = (within[None, :] < limits[first:last, None]).astype(jnp.float32)[:, None, :]
                parts.append(attend_packets(q3, got[first:last], keep, scale_factor))
            return combine(parts, rows_dev)

        attention = jnp.concatenate(
            [half(got_a, limit_a, 0, heads_a), half(got_b, limit_b, heads_a, heads_here)], axis=1
        )
        partial = jnp.dot(attention, out_weight, preferred_element_type=jnp.float32)
        rows_out = hidden.shape[0]
        side = lax.axis_index("tp")
        n_tp = rows_dev // rows_out
        pieces = partial.reshape(n_tp, rows_out, partial.shape[1])
        own = jnp.take(pieces, side, axis=0)
        other = jnp.take(pieces, 1 - side, axis=0).astype(jnp.bfloat16)
        came = lax.ppermute(other, "tp", [(0, 1), (1, 0)])
        summed = own + came.astype(jnp.float32)
        return (hidden.astype(jnp.float32) + gate_scale * summed).astype(jnp.bfloat16)

    placed = (
        P(("seq", "tp"), None),
        P("seq", "tp"),
        P("seq", "tp"),
        P("seq", "tp"),
        P(),
        P("tp", None),
        P("seq"),
        P("seq"),
    )
    return jax.shard_map(
        on_device, mesh=mesh, in_specs=placed, out_specs=P(("seq", "tp"), None), check_vma=False
    )
```

```python
import math

import jax
import jax.numpy as jnp
from jax import lax
from jax.sharding import PartitionSpec as P

HEAD = 128
neg_large = -1e30


def snake_ring(chips):
    half = chips // 2
    return [2 * a for a in range(half)] + [2 * a + 1 for a in reversed(range(half))]


def build(n_seq):
    chips = n_seq // 2
    ring = snake_ring(chips)
    half = chips // 2
    forward = [(ring[p] * 2 + c, ring[(p + 1) % chips] * 2 + c) for p in range(chips) for c in range(2)]
    backward = [(ring[(p + 1) % chips] * 2 + c, ring[p] * 2 + c) for p in range(chips) for c in range(2)]
    swap = [(i, i ^ 1) for i in range(n_seq)]

    def chip_at(pos):
        return jnp.where(pos < half, 2 * pos, 2 * (chips - 1 - pos) + 1)

    def gather_ring(packet_a, packet_b, me):
        chip = me // 2
        core = me % 2
        pos = jnp.where(chip % 2 == 0, chip // 2, chips - 1 - chip // 2)
        got_a, got_b, ids_a, ids_b = [], [], [], []
        cur_a, cur_b = packet_a, packet_b
        for step in range(chips):
            if step > 0:
                cur_a = lax.ppermute(cur_a, "seq", forward)
                cur_b = lax.ppermute(cur_b, "seq", backward)
            src_a = chip_at((pos - step) % chips) * 2 + core
            src_b = chip_at((pos + step) % chips) * 2 + core
            mate_a = lax.ppermute(cur_a, "seq", swap)
            mate_b = lax.ppermute(cur_b, "seq", swap)
            got_a += [cur_a, mate_a]
            got_b += [cur_b, mate_b]
            ids_a += [src_a, src_a ^ 1]
            ids_b += [src_b, src_b ^ 1]
        return got_a, got_b, jnp.stack(ids_a), jnp.stack(ids_b)

    return gather_ring


def attend_part(queries_3d, keys, values, keeping, scale_factor):
    scores = (
        jnp.einsum("hqd,hkd->hqk", queries_3d, keys, preferred_element_type=jnp.float32)
        * scale_factor
    )
    masked = jnp.where(keeping[None, None, :], scores, neg_large)
    peak = jnp.max(masked, axis=2, keepdims=True)
    weights = jnp.where(keeping[None, None, :], jnp.exp(masked - peak), 0.0)
    totals = jnp.sum(weights, axis=2, keepdims=True)
    summed = jnp.einsum(
        "hqk,hkd->hqd", weights.astype(jnp.bfloat16), values, preferred_element_type=jnp.float32
    )
    return peak, totals, summed


def combine(parts, rows_dev):
    peak = parts[0][0]
    for part in parts[1:]:
        peak = jnp.maximum(peak, part[0])
    totals = 0.0
    summed = 0.0
    for part_peak, part_totals, part_summed in parts:
        factor = jnp.exp(part_peak - peak)
        totals = totals + factor * part_totals
        summed = summed + factor * part_summed
    result = (summed / totals).astype(jnp.bfloat16)
    return result.transpose(1, 0, 2).reshape(rows_dev, -1)


def solution(mesh):
    n_seq = mesh.shape["seq"]
    gather_ring = build(n_seq)

    def on_device(
        hidden, queries, key_rows, value_rows, gate_scale, out_weight, valid_count, assignment
    ):
        rows_dev = queries.shape[0]
        heads_here = queries.shape[1] // HEAD
        heads_a = heads_here // 2
        cut = heads_a * HEAD
        scale_factor = 1.0 / math.sqrt(HEAD)
        me = lax.axis_index("seq")
        rows_pad = (rows_dev + 1 + 7) // 8 * 8
        row_id = lax.broadcasted_iota(jnp.int32, (rows_pad - rows_dev, HEAD), 0)
        col_id = lax.broadcasted_iota(jnp.int32, (rows_pad - rows_dev, HEAD), 1)
        info = jnp.where(
            (row_id == 0) & (col_id == 0),
            valid_count[0],
            jnp.where((row_id == 0) & (col_id == 1), assignment[0], 0),
        ).astype(jnp.bfloat16)

        def head_major(lo, hi):
            both = jnp.concatenate([key_rows[:, lo * HEAD : hi * HEAD], value_rows[:, lo * HEAD : hi * HEAD]], axis=1)
            both = both.reshape(rows_dev, 2 * (hi - lo), HEAD).transpose(1, 0, 2)
            pad = jnp.broadcast_to(info[None], (2 * (hi - lo),) + info.shape)
            return jnp.concatenate([both, pad], axis=1)

        packet_a = head_major(0, heads_a)
        packet_b = head_major(heads_a, heads_here)
        got_a, got_b, ids_a, ids_b = gather_ring(packet_a, packet_b, me)
        chips = n_seq // 2
        known = chips // 2
        seen = 2 * (known + 1)
        heard = got_a[:seen] + got_b[:seen]
        heard_ids = jnp.concatenate([ids_a[:seen], ids_b[:seen]])
        extra = jnp.stack([g[0, rows_dev, :2] for g in heard]).astype(jnp.float32).astype(jnp.int32)
        counts_of, blocks_of = extra[:, 0], extra[:, 1]

        def limits_for(ids):
            clip = jnp.max(jnp.where(ids[:, None] == heard_ids[None, :], blocks_of[None, :], -1), axis=1)
            return jnp.max(jnp.where(clip[:, None] == heard_ids[None, :], counts_of[None, :], -1), axis=1)

        limit_a = limits_for(ids_a)
        limit_b = limits_for(ids_b)
        within = jnp.arange(rows_pad, dtype=jnp.int32)
        phases = [(0, known + 1), (known + 1, chips - 1), (chips - 1, chips)]
        phases = [(2 * lo, 2 * hi) for lo, hi in phases if hi > lo]

        anchor = 2 * max(chips - 2, 0)
        early = 2 * (chips - 1)
        held_a, held_b, _ = lax.optimization_barrier(
            (got_a[:early], got_b[:early], (got_a[anchor], got_b[anchor]))
        )
        got_a = list(held_a) + got_a[early:]
        got_b = list(held_b) + got_b[early:]

        rows_out = hidden.shape[0]
        side = lax.axis_index("tp")
        n_tp = rows_dev // rows_out

        def half(got, limits, lo, hi, which):
            q3 = queries.reshape(n_tp, rows_out, queries.shape[1])
            q3 = jnp.take(q3, which, axis=0)[:, lo * HEAD : hi * HEAD]
            q3 = q3.reshape(rows_out, hi - lo, HEAD).transpose(1, 0, 2)
            parts = []
            for first, last in phases:
                stack = jnp.concatenate(got[first:last], axis=1)
                keys = stack[: hi - lo]
                values = stack[hi - lo :]
                keeping = (within[None, :] < limits[first:last, None]).reshape(-1)
                parts.append(attend_part(q3, keys, values, keeping, scale_factor))
            return combine(parts, rows_out)

        def attention_rows(which):
            return jnp.concatenate(
                [half(got_a, limit_a, 0, heads_a, which), half(got_b, limit_b, heads_a, heads_here, which)],
                axis=1,
            )

        other = jnp.dot(attention_rows(1 - side), out_weight, preferred_element_type=jnp.float32)
        other = other.astype(jnp.bfloat16)
        came = lax.ppermute(other, "tp", [(0, 1), (1, 0)])
        attention_own = attention_rows(side)
        own = jnp.dot(attention_own, out_weight, preferred_element_type=jnp.float32)
        summed = own + came.astype(jnp.float32)
        return (hidden.astype(jnp.float32) + gate_scale * summed).astype(jnp.bfloat16)

    placed = (
        P(("seq", "tp"), None),
        P("seq", "tp"),
        P("seq", "tp"),
        P("seq", "tp"),
        P(),
        P("tp", None),
        P("seq"),
        P("seq"),
    )
    return jax.shard_map(
        on_device, mesh=mesh, in_specs=placed, out_specs=P(("seq", "tp"), None), check_vma=False
    )
```

```python
import math

import jax
import jax.numpy as jnp
from jax import lax
from jax.experimental import pallas as pl
from jax.experimental.pallas import tpu as pltpu
from jax.sharding import PartitionSpec as P

HEAD = 128
neg_large = -1e30


def snake_ring(chips):
    half = chips // 2
    return [2 * a for a in range(half)] + [2 * a + 1 for a in reversed(range(half))]


def build(n_seq):
    chips = n_seq // 2
    ring = snake_ring(chips)
    half = chips // 2
    forward = [(ring[p] * 2 + c, ring[(p + 1) % chips] * 2 + c) for p in range(chips) for c in range(2)]
    backward = [(ring[(p + 1) % chips] * 2 + c, ring[p] * 2 + c) for p in range(chips) for c in range(2)]
    swap = [(i, i ^ 1) for i in range(n_seq)]

    def chip_at(pos):
        return jnp.where(pos < half, 2 * pos, 2 * (chips - 1 - pos) + 1)

    def gather_ring(packet_a, packet_b, me):
        chip = me // 2
        core = me % 2
        pos = jnp.where(chip % 2 == 0, chip // 2, chips - 1 - chip // 2)
        got_a, got_b, ids_a, ids_b = [], [], [], []
        cur_a, cur_b = packet_a, packet_b
        for step in range(chips):
            if step > 0:
                cur_a = lax.ppermute(cur_a, "seq", forward)
                cur_b = lax.ppermute(cur_b, "seq", backward)
            src_a = chip_at((pos - step) % chips) * 2 + core
            src_b = chip_at((pos + step) % chips) * 2 + core
            mate_a = lax.ppermute(cur_a, "seq", swap)
            mate_b = lax.ppermute(cur_b, "seq", swap)
            got_a += [cur_a, mate_a]
            got_b += [cur_b, mate_b]
            ids_a += [src_a, src_a ^ 1]
            ids_b += [src_b, src_b ^ 1]
        return got_a, got_b, jnp.stack(ids_a), jnp.stack(ids_b)

    return gather_ring


def attend_part(queries_3d, keys, values, keeping, scale_factor):
    scores = (
        jnp.einsum("hqd,hkd->hqk", queries_3d, keys, preferred_element_type=jnp.float32)
        * scale_factor
    )
    masked = jnp.where(keeping[None, None, :], scores, neg_large)
    peak = jnp.max(masked, axis=2, keepdims=True)
    weights = jnp.where(keeping[None, None, :], jnp.exp(masked - peak), 0.0)
    totals = jnp.sum(weights, axis=2, keepdims=True)
    summed = jnp.einsum(
        "hqk,hkd->hqd", weights.astype(jnp.bfloat16), values, preferred_element_type=jnp.float32
    )
    return peak, totals, summed


def join_packets(packets, interpret=False):
    count = len(packets)
    heads, rows, width = packets[0].shape

    def kernel(*refs):
        sources, target, sems = refs[:count], refs[count], refs[count + 1]
        copies = [
            pltpu.make_async_copy(sources[i], target.at[:, i * rows : (i + 1) * rows, :], sems.at[i])
            for i in range(count)
        ]
        for copy in copies:
            copy.start()
        for copy in copies:
            copy.wait()

    return pl.pallas_call(
        kernel,
        out_shape=jax.ShapeDtypeStruct((heads, count * rows, width), packets[0].dtype),
        in_specs=[pl.BlockSpec(memory_space=pl.ANY)] * count,
        out_specs=pl.BlockSpec(memory_space=pl.ANY),
        scratch_shapes=[pltpu.SemaphoreType.DMA((count,))],
        interpret=interpret,
    )(*packets)


def combine(parts, rows_dev):
    peak = parts[0][0]
    for part in parts[1:]:
        peak = jnp.maximum(peak, part[0])
    totals = 0.0
    summed = 0.0
    for part_peak, part_totals, part_summed in parts:
        factor = jnp.exp(part_peak - peak)
        totals = totals + factor * part_totals
        summed = summed + factor * part_summed
    result = (summed / totals).astype(jnp.bfloat16)
    return result.transpose(1, 0, 2).reshape(rows_dev, -1)


def solution(mesh):
    n_seq = mesh.shape["seq"]
    gather_ring = build(n_seq)

    def on_device(
        hidden, queries, key_rows, value_rows, gate_scale, out_weight, valid_count, assignment
    ):
        rows_dev = queries.shape[0]
        heads_here = queries.shape[1] // HEAD
        heads_a = heads_here // 2
        cut = heads_a * HEAD
        scale_factor = 1.0 / math.sqrt(HEAD)
        me = lax.axis_index("seq")
        rows_pad = (rows_dev + 1 + 7) // 8 * 8
        row_id = lax.broadcasted_iota(jnp.int32, (rows_pad - rows_dev, HEAD), 0)
        col_id = lax.broadcasted_iota(jnp.int32, (rows_pad - rows_dev, HEAD), 1)
        info = jnp.where(
            (row_id == 0) & (col_id == 0),
            valid_count[0],
            jnp.where((row_id == 0) & (col_id == 1), assignment[0], 0),
        ).astype(jnp.bfloat16)

        def head_major(lo, hi):
            both = jnp.concatenate([key_rows[:, lo * HEAD : hi * HEAD], value_rows[:, lo * HEAD : hi * HEAD]], axis=1)
            both = both.reshape(rows_dev, 2 * (hi - lo), HEAD).transpose(1, 0, 2)
            pad = jnp.broadcast_to(info[None], (2 * (hi - lo),) + info.shape)
            return jnp.concatenate([both, pad], axis=1)

        packet_a = head_major(0, heads_a)
        packet_b = head_major(heads_a, heads_here)
        got_a, got_b, ids_a, ids_b = gather_ring(packet_a, packet_b, me)
        chips = n_seq // 2
        known = chips // 2
        seen = 2 * (known + 1)
        heard = got_a[:seen] + got_b[:seen]
        heard_ids = jnp.concatenate([ids_a[:seen], ids_b[:seen]])
        extra = jnp.stack([g[0, rows_dev, :2] for g in heard]).astype(jnp.float32).astype(jnp.int32)
        counts_of, blocks_of = extra[:, 0], extra[:, 1]

        def limits_for(ids):
            clip = jnp.max(jnp.where(ids[:, None] == heard_ids[None, :], blocks_of[None, :], -1), axis=1)
            return jnp.max(jnp.where(clip[:, None] == heard_ids[None, :], counts_of[None, :], -1), axis=1)

        limit_a = limits_for(ids_a)
        limit_b = limits_for(ids_b)
        within = jnp.arange(rows_pad, dtype=jnp.int32)
        phases = [(0, known + 1), (known + 1, chips - 1), (chips - 1, chips)]
        phases = [(2 * lo, 2 * hi) for lo, hi in phases if hi > lo]

        anchor = 2 * max(chips - 2, 0)
        early = 2 * (chips - 1)
        held_a, held_b, _ = lax.optimization_barrier(
            (got_a[:early], got_b[:early], (got_a[anchor], got_b[anchor]))
        )
        got_a = list(held_a) + got_a[early:]
        got_b = list(held_b) + got_b[early:]

        rows_out = hidden.shape[0]
        side = lax.axis_index("tp")
        n_tp = rows_dev // rows_out

        stacks_a = [join_packets(got_a[first:last]) for first, last in phases]
        stacks_b = [join_packets(got_b[first:last]) for first, last in phases]

        def half(stacks, limits, lo, hi, which):
            q3 = queries.reshape(n_tp, rows_out, queries.shape[1])
            q3 = jnp.take(q3, which, axis=0)[:, lo * HEAD : hi * HEAD]
            q3 = q3.reshape(rows_out, hi - lo, HEAD).transpose(1, 0, 2)
            parts = []
            for (first, last), stack in zip(phases, stacks):
                keys = stack[: hi - lo]
                values = stack[hi - lo :]
                keeping = (within[None, :] < limits[first:last, None]).reshape(-1)
                parts.append(attend_part(q3, keys, values, keeping, scale_factor))
            return combine(parts, rows_out)

        def attention_rows(which):
            return jnp.concatenate(
                [half(stacks_a, limit_a, 0, heads_a, which), half(stacks_b, limit_b, heads_a, heads_here, which)],
                axis=1,
            )

        other = jnp.dot(attention_rows(1 - side), out_weight, preferred_element_type=jnp.float32)
        other = other.astype(jnp.bfloat16)
        came = lax.ppermute(other, "tp", [(0, 1), (1, 0)])
        attention_own = attention_rows(side)
        own = jnp.dot(attention_own, out_weight, preferred_element_type=jnp.float32)
        summed = own + came.astype(jnp.float32)
        return (hidden.astype(jnp.float32) + gate_scale * summed).astype(jnp.bfloat16)

    placed = (
        P(("seq", "tp"), None),
        P("seq", "tp"),
        P("seq", "tp"),
        P("seq", "tp"),
        P(),
        P("tp", None),
        P("seq"),
        P("seq"),
    )
    return jax.shard_map(
        on_device, mesh=mesh, in_specs=placed, out_specs=P(("seq", "tp"), None), check_vma=False
    )
```

```python
import math

import jax
import jax.numpy as jnp
from jax import lax
from jax.sharding import PartitionSpec as P

HEAD = 128
neg_large = -1e30


def snake_ring(chips):
    half = chips // 2
    return [2 * a for a in range(half)] + [2 * a + 1 for a in reversed(range(half))]


def build(n_seq):
    chips = n_seq // 2
    ring = snake_ring(chips)
    half = chips // 2
    forward = [(ring[p] * 2 + c, ring[(p + 1) % chips] * 2 + c) for p in range(chips) for c in range(2)]
    backward = [(ring[(p + 1) % chips] * 2 + c, ring[p] * 2 + c) for p in range(chips) for c in range(2)]
    swap = [(i, i ^ 1) for i in range(n_seq)]

    def chip_at(pos):
        return jnp.where(pos < half, 2 * pos, 2 * (chips - 1 - pos) + 1)

    def gather_ring(packet_a, packet_b, me):
        chip = me // 2
        core = me % 2
        pos = jnp.where(chip % 2 == 0, chip // 2, chips - 1 - chip // 2)
        got_a, got_b, ids_a, ids_b = [], [], [], []
        cur_a, cur_b = packet_a, packet_b
        for step in range(chips):
            if step > 0:
                cur_a = lax.ppermute(cur_a, "seq", forward)
                cur_b = lax.ppermute(cur_b, "seq", backward)
            src_a = chip_at((pos - step) % chips) * 2 + core
            src_b = chip_at((pos + step) % chips) * 2 + core
            mate_a = lax.ppermute(cur_a, "seq", swap)
            mate_b = lax.ppermute(cur_b, "seq", swap)
            got_a += [cur_a, mate_a]
            got_b += [cur_b, mate_b]
            ids_a += [src_a, src_a ^ 1]
            ids_b += [src_b, src_b ^ 1]
        return got_a, got_b, jnp.stack(ids_a), jnp.stack(ids_b)

    return gather_ring


def attend_part(queries_3d, keys, values, keeping, scale_factor):
    scores = (
        jnp.einsum("hqd,hkd->hqk", queries_3d, keys, preferred_element_type=jnp.float32)
        * scale_factor
    )
    masked = jnp.where(keeping[None, None, :], scores, neg_large)
    peak = jnp.max(masked, axis=2, keepdims=True)
    weights = jnp.where(keeping[None, None, :], jnp.exp(masked - peak), 0.0)
    totals = jnp.sum(weights, axis=2, keepdims=True)
    summed = jnp.einsum(
        "hqk,hkd->hqd", weights.astype(jnp.bfloat16), values, preferred_element_type=jnp.float32
    )
    return peak, totals, summed


def combine(parts, rows_dev):
    peak = parts[0][0]
    for part in parts[1:]:
        peak = jnp.maximum(peak, part[0])
    totals = 0.0
    summed = 0.0
    for part_peak, part_totals, part_summed in parts:
        factor = jnp.exp(part_peak - peak)
        totals = totals + factor * part_totals
        summed = summed + factor * part_summed
    result = (summed / totals).astype(jnp.bfloat16)
    return result.transpose(1, 0, 2).reshape(rows_dev, -1)


def solution(mesh):
    n_seq = mesh.shape["seq"]
    gather_ring = build(n_seq)

    def on_device(
        hidden, queries, key_rows, value_rows, gate_scale, out_weight, valid_count, assignment
    ):
        rows_dev = queries.shape[0]
        heads_here = queries.shape[1] // HEAD
        heads_a = heads_here // 2
        cut = heads_a * HEAD
        scale_factor = 1.0 / math.sqrt(HEAD)
        me = lax.axis_index("seq")
        rows_pad = (rows_dev + 1 + 7) // 8 * 8
        row_id = lax.broadcasted_iota(jnp.int32, (rows_pad - rows_dev, HEAD), 0)
        col_id = lax.broadcasted_iota(jnp.int32, (rows_pad - rows_dev, HEAD), 1)
        info = jnp.where(
            (row_id == 0) & (col_id == 0),
            valid_count[0],
            jnp.where((row_id == 0) & (col_id == 1), assignment[0], 0),
        ).astype(jnp.bfloat16)

        def head_major(lo, hi):
            both = jnp.concatenate([key_rows[:, lo * HEAD : hi * HEAD], value_rows[:, lo * HEAD : hi * HEAD]], axis=1)
            both = both.reshape(rows_dev, 2 * (hi - lo), HEAD).transpose(1, 0, 2)
            pad = jnp.broadcast_to(info[None], (2 * (hi - lo),) + info.shape)
            return jnp.concatenate([both, pad], axis=1)

        packet_a = head_major(0, heads_a)
        packet_b = head_major(heads_a, heads_here)
        got_a, got_b, ids_a, ids_b = gather_ring(packet_a, packet_b, me)
        chips = n_seq // 2
        known = chips // 2
        seen = 2 * (known + 1)
        heard = got_a[:seen] + got_b[:seen]
        heard_ids = jnp.concatenate([ids_a[:seen], ids_b[:seen]])
        extra = jnp.stack([g[0, rows_dev, :2] for g in heard]).astype(jnp.float32).astype(jnp.int32)
        counts_of, blocks_of = extra[:, 0], extra[:, 1]

        def limits_for(ids):
            clip = jnp.max(jnp.where(ids[:, None] == heard_ids[None, :], blocks_of[None, :], -1), axis=1)
            return jnp.max(jnp.where(clip[:, None] == heard_ids[None, :], counts_of[None, :], -1), axis=1)

        limit_a = limits_for(ids_a)
        limit_b = limits_for(ids_b)
        within = jnp.arange(rows_pad, dtype=jnp.int32)
        phases = [(0, known + 1), (known + 1, chips - 1), (chips - 1, chips)]
        phases = [(2 * lo, 2 * hi) for lo, hi in phases if hi > lo]

        anchor = 2 * min(known + 1, chips - 1)
        early = 2 * (known + 1)
        held_a, held_b, _ = lax.optimization_barrier(
            (got_a[:early], got_b[:early], (got_a[anchor], got_b[anchor]))
        )
        got_a = list(held_a) + got_a[early:]
        got_b = list(held_b) + got_b[early:]

        rows_out = hidden.shape[0]
        side = lax.axis_index("tp")
        n_tp = rows_dev // rows_out

        def half(got, limits, lo, hi, which):
            q3 = queries.reshape(n_tp, rows_out, queries.shape[1])
            q3 = jnp.take(q3, which, axis=0)[:, lo * HEAD : hi * HEAD]
            q3 = q3.reshape(rows_out, hi - lo, HEAD).transpose(1, 0, 2)
            parts = []
            for first, last in phases:
                stack = jnp.concatenate(got[first:last], axis=1)
                keys = stack[: hi - lo]
                values = stack[hi - lo :]
                keeping = (within[None, :] < limits[first:last, None]).reshape(-1)
                parts.append(attend_part(q3, keys, values, keeping, scale_factor))
            return combine(parts, rows_out)

        def attention_rows(which):
            return jnp.concatenate(
                [half(got_a, limit_a, 0, heads_a, which), half(got_b, limit_b, heads_a, heads_here, which)],
                axis=1,
            )

        other = jnp.dot(attention_rows(1 - side), out_weight, preferred_element_type=jnp.float32)
        other = other.astype(jnp.bfloat16)
        came = lax.ppermute(other, "tp", [(0, 1), (1, 0)])
        attention_own = attention_rows(side)
        own = jnp.dot(attention_own, out_weight, preferred_element_type=jnp.float32)
        summed = own + came.astype(jnp.float32)
        return (hidden.astype(jnp.float32) + gate_scale * summed).astype(jnp.bfloat16)

    placed = (
        P(("seq", "tp"), None),
        P("seq", "tp"),
        P("seq", "tp"),
        P("seq", "tp"),
        P(),
        P("tp", None),
        P("seq"),
        P("seq"),
    )
    return jax.shard_map(
        on_device, mesh=mesh, in_specs=placed, out_specs=P(("seq", "tp"), None), check_vma=False
    )
```

```python
import math

import jax
import jax.numpy as jnp
from jax import lax
from jax.sharding import PartitionSpec as P

HEAD = 128
neg_large = -1e30


def snake_ring(chips):
    half = chips // 2
    return [2 * a for a in range(half)] + [2 * a + 1 for a in reversed(range(half))]


def build(n_seq):
    chips = n_seq // 2
    ring = snake_ring(chips)
    half = chips // 2
    forward = [(ring[p] * 2 + c, ring[(p + 1) % chips] * 2 + c) for p in range(chips) for c in range(2)]
    backward = [(ring[(p + 1) % chips] * 2 + c, ring[p] * 2 + c) for p in range(chips) for c in range(2)]
    swap = [(i, i ^ 1) for i in range(n_seq)]

    def chip_at(pos):
        return jnp.where(pos < half, 2 * pos, 2 * (chips - 1 - pos) + 1)

    def gather_ring(packet_a, packet_b, me):
        chip = me // 2
        core = me % 2
        pos = jnp.where(chip % 2 == 0, chip // 2, chips - 1 - chip // 2)
        got_a, got_b, ids_a, ids_b = [], [], [], []
        cur_a, cur_b = packet_a, packet_b
        for step in range(chips):
            if step > 0:
                cur_a = lax.ppermute(cur_a, "seq", forward)
                cur_b = lax.ppermute(cur_b, "seq", backward)
            src_a = chip_at((pos - step) % chips) * 2 + core
            src_b = chip_at((pos + step) % chips) * 2 + core
            mate_a = lax.ppermute(cur_a, "seq", swap)
            mate_b = lax.ppermute(cur_b, "seq", swap)
            got_a += [cur_a, mate_a]
            got_b += [cur_b, mate_b]
            ids_a += [src_a, src_a ^ 1]
            ids_b += [src_b, src_b ^ 1]
        return got_a, got_b, jnp.stack(ids_a), jnp.stack(ids_b)

    return gather_ring


def attend_part(queries_3d, keys, values, keeping, scale_factor):
    scores = (
        jnp.einsum("hqd,hkd->hqk", queries_3d, keys, preferred_element_type=jnp.float32)
        * scale_factor
    )
    masked = jnp.where(keeping[None, None, :], scores, neg_large)
    peak = jnp.max(masked, axis=2, keepdims=True)
    weights = jnp.where(keeping[None, None, :], jnp.exp(masked - peak), 0.0)
    totals = jnp.sum(weights, axis=2, keepdims=True)
    summed = jnp.einsum(
        "hqk,hkd->hqd", weights.astype(jnp.bfloat16), values, preferred_element_type=jnp.float32
    )
    return peak, totals, summed


def combine(parts, rows_dev):
    peak = parts[0][0]
    for part in parts[1:]:
        peak = jnp.maximum(peak, part[0])
    totals = 0.0
    summed = 0.0
    for part_peak, part_totals, part_summed in parts:
        factor = jnp.exp(part_peak - peak)
        totals = totals + factor * part_totals
        summed = summed + factor * part_summed
    result = (summed / totals).astype(jnp.bfloat16)
    return result.transpose(1, 0, 2).reshape(rows_dev, -1)


def solution(mesh):
    n_seq = mesh.shape["seq"]
    gather_ring = build(n_seq)

    def on_device(
        hidden, queries, key_rows, value_rows, gate_scale, out_weight, valid_count, assignment
    ):
        rows_dev = queries.shape[0]
        heads_here = queries.shape[1] // HEAD
        heads_a = heads_here // 2
        cut = heads_a * HEAD
        scale_factor = 1.0 / math.sqrt(HEAD)
        me = lax.axis_index("seq")
        rows_pad = (rows_dev + 1 + 7) // 8 * 8
        row_id = lax.broadcasted_iota(jnp.int32, (rows_pad - rows_dev, HEAD), 0)
        col_id = lax.broadcasted_iota(jnp.int32, (rows_pad - rows_dev, HEAD), 1)
        info = jnp.where(
            (row_id == 0) & (col_id == 0),
            valid_count[0],
            jnp.where((row_id == 0) & (col_id == 1), assignment[0], 0),
        ).astype(jnp.bfloat16)

        def head_major(lo, hi):
            both = jnp.concatenate([key_rows[:, lo * HEAD : hi * HEAD], value_rows[:, lo * HEAD : hi * HEAD]], axis=1)
            both = both.reshape(rows_dev, 2 * (hi - lo), HEAD).transpose(1, 0, 2)
            pad = jnp.broadcast_to(info[None], (2 * (hi - lo),) + info.shape)
            return jnp.concatenate([both, pad], axis=1)

        packet_a = head_major(0, heads_a)
        packet_b = head_major(heads_a, heads_here)
        got_a, got_b, ids_a, ids_b = gather_ring(packet_a, packet_b, me)
        chips = n_seq // 2
        known = chips // 2
        seen = 2 * (known + 1)
        heard = got_a[:seen] + got_b[:seen]
        heard_ids = jnp.concatenate([ids_a[:seen], ids_b[:seen]])
        extra = jnp.stack([g[0, rows_dev, :2] for g in heard]).astype(jnp.float32).astype(jnp.int32)
        counts_of, blocks_of = extra[:, 0], extra[:, 1]

        def limits_for(ids):
            clip = jnp.max(jnp.where(ids[:, None] == heard_ids[None, :], blocks_of[None, :], -1), axis=1)
            return jnp.max(jnp.where(clip[:, None] == heard_ids[None, :], counts_of[None, :], -1), axis=1)

        limit_a = limits_for(ids_a)
        limit_b = limits_for(ids_b)
        within = jnp.arange(rows_pad, dtype=jnp.int32)
        phases = [(0, known + 1), (known + 1, chips - 1), (chips - 1, chips)]
        phases = [(2 * lo, 2 * hi) for lo, hi in phases if hi > lo]

        anchor = 2 * max(chips - 2, 0)
        early = 2 * (chips - 1)
        held_a, held_b, _ = lax.optimization_barrier(
            (got_a[:early], got_b[:early], (got_a[anchor], got_b[anchor]))
        )
        got_a = list(held_a) + got_a[early:]
        got_b = list(held_b) + got_b[early:]

        rows_out = hidden.shape[0]
        side = lax.axis_index("tp")
        n_tp = rows_dev // rows_out

        def half(got, limits, lo, hi, which):
            q3 = queries.reshape(n_tp, rows_out, queries.shape[1])
            q3 = jnp.take(q3, which, axis=0)[:, lo * HEAD : hi * HEAD]
            q3 = q3.reshape(rows_out, hi - lo, HEAD).transpose(1, 0, 2)
            parts = []
            for first, last in phases:
                stack = jnp.concatenate(got[first:last], axis=1)
                keys = stack[: hi - lo]
                values = stack[hi - lo :]
                keeping = (within[None, :] < limits[first:last, None]).reshape(-1)
                parts.append(attend_part(q3, keys, values, keeping, scale_factor))
            return combine(parts, rows_out)

        def attention_rows(which):
            return jnp.concatenate(
                [half(got_a, limit_a, 0, heads_a, which), half(got_b, limit_b, heads_a, heads_here, which)],
                axis=1,
            )

        other = jnp.dot(attention_rows(1 - side), out_weight, preferred_element_type=jnp.float32)
        other = other.astype(jnp.bfloat16)
        came = lax.ppermute(other, "tp", [(0, 1), (1, 0)])
        attention_own = attention_rows(side)
        own = jnp.dot(attention_own, out_weight, preferred_element_type=jnp.float32)
        own = lax.optimization_barrier(own)
        summed = own + came.astype(jnp.float32)
        return (hidden.astype(jnp.float32) + gate_scale * summed).astype(jnp.bfloat16)

    placed = (
        P(("seq", "tp"), None),
        P("seq", "tp"),
        P("seq", "tp"),
        P("seq", "tp"),
        P(),
        P("tp", None),
        P("seq"),
        P("seq"),
    )
    return jax.shard_map(
        on_device, mesh=mesh, in_specs=placed, out_specs=P(("seq", "tp"), None), check_vma=False
    )
```

```python
import math

import jax
import jax.numpy as jnp
from jax import lax
from jax.sharding import PartitionSpec as P

HEAD = 128
neg_large = -1e30


def snake_ring(chips):
    half = chips // 2
    return [2 * a for a in range(half)] + [2 * a + 1 for a in reversed(range(half))]


def build(n_seq):
    chips = n_seq // 2
    ring = snake_ring(chips)
    half = chips // 2
    forward = [(ring[p] * 2 + c, ring[(p + 1) % chips] * 2 + c) for p in range(chips) for c in range(2)]
    backward = [(ring[(p + 1) % chips] * 2 + c, ring[p] * 2 + c) for p in range(chips) for c in range(2)]
    swap = [(i, i ^ 1) for i in range(n_seq)]

    def chip_at(pos):
        return jnp.where(pos < half, 2 * pos, 2 * (chips - 1 - pos) + 1)

    def gather_ring(packet_a, packet_b, me):
        chip = me // 2
        core = me % 2
        pos = jnp.where(chip % 2 == 0, chip // 2, chips - 1 - chip // 2)
        got_a, got_b, ids_a, ids_b = [], [], [], []
        cur_a, cur_b = packet_a, packet_b
        for step in range(chips):
            if step > 0:
                cur_a = lax.ppermute(cur_a, "seq", forward)
                cur_b = lax.ppermute(cur_b, "seq", backward)
            src_a = chip_at((pos - step) % chips) * 2 + core
            src_b = chip_at((pos + step) % chips) * 2 + core
            mate_a = lax.ppermute(cur_a, "seq", swap)
            mate_b = lax.ppermute(cur_b, "seq", swap)
            got_a += [cur_a, mate_a]
            got_b += [cur_b, mate_b]
            ids_a += [src_a, src_a ^ 1]
            ids_b += [src_b, src_b ^ 1]
        return got_a, got_b, jnp.stack(ids_a), jnp.stack(ids_b)

    return gather_ring


def attend_part(queries_3d, keys, values, keeping, scale_factor):
    scores = (
        jnp.einsum("hqd,nhkd->hqnk", queries_3d, keys, preferred_element_type=jnp.float32)
        * scale_factor
    )
    masked = jnp.where(keeping[None, None], scores, neg_large)
    peak = jnp.max(masked, axis=(2, 3))[:, :, None]
    weights = jnp.where(keeping[None, None], jnp.exp(masked - peak[:, :, :, None]), 0.0)
    totals = jnp.sum(weights, axis=(2, 3))[:, :, None]
    summed = jnp.einsum(
        "hqnk,nhkd->hqd", weights.astype(jnp.bfloat16), values, preferred_element_type=jnp.float32
    )
    return peak, totals, summed


def combine(parts, rows_dev):
    peak = parts[0][0]
    for part in parts[1:]:
        peak = jnp.maximum(peak, part[0])
    totals = 0.0
    summed = 0.0
    for part_peak, part_totals, part_summed in parts:
        factor = jnp.exp(part_peak - peak)
        totals = totals + factor * part_totals
        summed = summed + factor * part_summed
    result = (summed / totals).astype(jnp.bfloat16)
    return result.transpose(1, 0, 2).reshape(rows_dev, -1)


def solution(mesh):
    n_seq = mesh.shape["seq"]
    gather_ring = build(n_seq)

    def on_device(
        hidden, queries, key_rows, value_rows, gate_scale, out_weight, valid_count, assignment
    ):
        rows_dev = queries.shape[0]
        heads_here = queries.shape[1] // HEAD
        heads_a = heads_here // 2
        cut = heads_a * HEAD
        scale_factor = 1.0 / math.sqrt(HEAD)
        me = lax.axis_index("seq")
        rows_pad = (rows_dev + 1 + 7) // 8 * 8
        row_id = lax.broadcasted_iota(jnp.int32, (rows_pad - rows_dev, HEAD), 0)
        col_id = lax.broadcasted_iota(jnp.int32, (rows_pad - rows_dev, HEAD), 1)
        info = jnp.where(
            (row_id == 0) & (col_id == 0),
            valid_count[0],
            jnp.where((row_id == 0) & (col_id == 1), assignment[0], 0),
        ).astype(jnp.bfloat16)

        def head_major(lo, hi):
            both = jnp.concatenate([key_rows[:, lo * HEAD : hi * HEAD], value_rows[:, lo * HEAD : hi * HEAD]], axis=1)
            both = both.reshape(rows_dev, 2 * (hi - lo), HEAD).transpose(1, 0, 2)
            pad = jnp.broadcast_to(info[None], (2 * (hi - lo),) + info.shape)
            return jnp.concatenate([both, pad], axis=1)

        packet_a = head_major(0, heads_a)
        packet_b = head_major(heads_a, heads_here)
        got_a, got_b, ids_a, ids_b = gather_ring(packet_a, packet_b, me)
        chips = n_seq // 2
        known = chips // 2
        seen = 2 * (known + 1)
        heard = got_a[:seen] + got_b[:seen]
        heard_ids = jnp.concatenate([ids_a[:seen], ids_b[:seen]])
        extra = jnp.stack([g[0, rows_dev, :2] for g in heard]).astype(jnp.float32).astype(jnp.int32)
        counts_of, blocks_of = extra[:, 0], extra[:, 1]

        def limits_for(ids):
            clip = jnp.max(jnp.where(ids[:, None] == heard_ids[None, :], blocks_of[None, :], -1), axis=1)
            return jnp.max(jnp.where(clip[:, None] == heard_ids[None, :], counts_of[None, :], -1), axis=1)

        limit_a = limits_for(ids_a)
        limit_b = limits_for(ids_b)
        within = jnp.arange(rows_pad, dtype=jnp.int32)
        phases = [(0, known + 1), (known + 1, chips - 1), (chips - 1, chips)]
        phases = [(2 * lo, 2 * hi) for lo, hi in phases if hi > lo]

        anchor = 2 * max(chips - 2, 0)
        early = 2 * (chips - 1)
        held_a, held_b, _ = lax.optimization_barrier(
            (got_a[:early], got_b[:early], (got_a[anchor], got_b[anchor]))
        )
        got_a = list(held_a) + got_a[early:]
        got_b = list(held_b) + got_b[early:]

        rows_out = hidden.shape[0]
        side = lax.axis_index("tp")
        n_tp = rows_dev // rows_out

        def half(got, limits, lo, hi, which):
            q3 = queries.reshape(n_tp, rows_out, queries.shape[1])
            q3 = jnp.take(q3, which, axis=0)[:, lo * HEAD : hi * HEAD]
            q3 = q3.reshape(rows_out, hi - lo, HEAD).transpose(1, 0, 2)
            parts = []
            for first, last in phases:
                stack = jnp.stack(got[first:last])
                keys = stack[:, : hi - lo]
                values = stack[:, hi - lo :]
                keeping = within[None, :] < limits[first:last, None]
                parts.append(attend_part(q3, keys, values, keeping, scale_factor))
            return combine(parts, rows_out)

        def attention_rows(which):
            return jnp.concatenate(
                [half(got_a, limit_a, 0, heads_a, which), half(got_b, limit_b, heads_a, heads_here, which)],
                axis=1,
            )

        other = jnp.dot(attention_rows(1 - side), out_weight, preferred_element_type=jnp.float32)
        other = other.astype(jnp.bfloat16)
        came = lax.ppermute(other, "tp", [(0, 1), (1, 0)])
        attention_own = attention_rows(side)
        own = jnp.dot(attention_own, out_weight, preferred_element_type=jnp.float32)
        own = lax.optimization_barrier(own)
        summed = own + came.astype(jnp.float32)
        return (hidden.astype(jnp.float32) + gate_scale * summed).astype(jnp.bfloat16)

    placed = (
        P(("seq", "tp"), None),
        P("seq", "tp"),
        P("seq", "tp"),
        P("seq", "tp"),
        P(),
        P("tp", None),
        P("seq"),
        P("seq"),
    )
    return jax.shard_map(
        on_device, mesh=mesh, in_specs=placed, out_specs=P(("seq", "tp"), None), check_vma=False
    )
```

```python
import math

import jax
import jax.numpy as jnp
from jax import lax
from jax.sharding import PartitionSpec as P

HEAD = 128
neg_large = -1e30


def snake_ring(chips):
    half = chips // 2
    return [2 * a for a in range(half)] + [2 * a + 1 for a in reversed(range(half))]


def build(n_seq):
    chips = n_seq // 2
    ring = snake_ring(chips)
    half = chips // 2
    forward = [(ring[p] * 2 + c, ring[(p + 1) % chips] * 2 + c) for p in range(chips) for c in range(2)]
    backward = [(ring[(p + 1) % chips] * 2 + c, ring[p] * 2 + c) for p in range(chips) for c in range(2)]
    swap = [(i, i ^ 1) for i in range(n_seq)]

    def chip_at(pos):
        return jnp.where(pos < half, 2 * pos, 2 * (chips - 1 - pos) + 1)

    def gather_ring(packet_a, packet_b, me):
        chip = me // 2
        core = me % 2
        pos = jnp.where(chip % 2 == 0, chip // 2, chips - 1 - chip // 2)
        got_a, got_b, ids_a, ids_b = [], [], [], []
        cur_a, cur_b = packet_a, packet_b
        for step in range(chips):
            if step > 0:
                cur_a = lax.ppermute(cur_a, "seq", forward)
                cur_b = lax.ppermute(cur_b, "seq", backward)
            src_a = chip_at((pos - step) % chips) * 2 + core
            src_b = chip_at((pos + step) % chips) * 2 + core
            mate_a = lax.ppermute(cur_a, "seq", swap)
            mate_b = lax.ppermute(cur_b, "seq", swap)
            got_a += [cur_a, mate_a]
            got_b += [cur_b, mate_b]
            ids_a += [src_a, src_a ^ 1]
            ids_b += [src_b, src_b ^ 1]
        return got_a, got_b, jnp.stack(ids_a), jnp.stack(ids_b)

    return gather_ring


def attend_part(queries_3d, keys, values, keeping, scale_factor):
    scores = (
        jnp.einsum("hqd,nhkd->hqnk", queries_3d, keys, preferred_element_type=jnp.float32)
        * scale_factor
    )
    masked = jnp.where(keeping[None, None], scores, neg_large)
    peak = jnp.max(masked, axis=(2, 3))[:, :, None]
    weights = jnp.where(keeping[None, None], jnp.exp(masked - peak[:, :, :, None]), 0.0)
    totals = jnp.sum(weights, axis=(2, 3))[:, :, None]
    summed = jnp.einsum(
        "hqnk,nhkd->hqd", weights.astype(jnp.bfloat16), values, preferred_element_type=jnp.float32
    )
    return peak, totals, summed


def combine(parts, rows_dev):
    peak = parts[0][0]
    for part in parts[1:]:
        peak = jnp.maximum(peak, part[0])
    totals = 0.0
    summed = 0.0
    for part_peak, part_totals, part_summed in parts:
        factor = jnp.exp(part_peak - peak)
        totals = totals + factor * part_totals
        summed = summed + factor * part_summed
    result = (summed / totals).astype(jnp.bfloat16)
    return result.transpose(1, 0, 2).reshape(rows_dev, -1)


def solution(mesh):
    n_seq = mesh.shape["seq"]
    gather_ring = build(n_seq)

    def on_device(
        hidden, queries, key_rows, value_rows, gate_scale, out_weight, valid_count, assignment
    ):
        rows_dev = queries.shape[0]
        heads_here = queries.shape[1] // HEAD
        heads_a = heads_here // 2
        cut = heads_a * HEAD
        scale_factor = 1.0 / math.sqrt(HEAD)
        me = lax.axis_index("seq")
        rows_pad = (rows_dev + 1 + 7) // 8 * 8
        row_id = lax.broadcasted_iota(jnp.int32, (rows_pad - rows_dev, HEAD), 0)
        col_id = lax.broadcasted_iota(jnp.int32, (rows_pad - rows_dev, HEAD), 1)
        info = jnp.where(
            (row_id == 0) & (col_id == 0),
            valid_count[0],
            jnp.where((row_id == 0) & (col_id == 1), assignment[0], 0),
        ).astype(jnp.bfloat16)

        def head_major(lo, hi):
            both = jnp.concatenate([key_rows[:, lo * HEAD : hi * HEAD], value_rows[:, lo * HEAD : hi * HEAD]], axis=1)
            both = both.reshape(rows_dev, 2 * (hi - lo), HEAD).transpose(1, 0, 2)
            pad = jnp.broadcast_to(info[None], (2 * (hi - lo),) + info.shape)
            return jnp.concatenate([both, pad], axis=1)

        packet_a = head_major(0, heads_a)
        packet_b = head_major(heads_a, heads_here)
        got_a, got_b, ids_a, ids_b = gather_ring(packet_a, packet_b, me)
        chips = n_seq // 2
        known = chips // 2
        seen = 2 * (known + 1)
        heard = got_a[:seen] + got_b[:seen]
        heard_ids = jnp.concatenate([ids_a[:seen], ids_b[:seen]])
        extra = jnp.stack([g[0, rows_dev, :2] for g in heard]).astype(jnp.float32).astype(jnp.int32)
        counts_of, blocks_of = extra[:, 0], extra[:, 1]

        def limits_for(ids):
            clip = jnp.max(jnp.where(ids[:, None] == heard_ids[None, :], blocks_of[None, :], -1), axis=1)
            return jnp.max(jnp.where(clip[:, None] == heard_ids[None, :], counts_of[None, :], -1), axis=1)

        limit_a = limits_for(ids_a)
        limit_b = limits_for(ids_b)
        within = jnp.arange(rows_pad, dtype=jnp.int32)
        phases = [(0, known + 1), (known + 1, chips - 1), (chips - 1, chips)]
        phases = [(2 * lo, 2 * hi) for lo, hi in phases if hi > lo]
        phases = phases[:-1] + [(phases[-1][0], phases[-1][0] + 1), (phases[-1][0] + 1, phases[-1][1])]

        anchor = 2 * max(chips - 2, 0)
        early = 2 * (chips - 1)
        held_a, held_b, _ = lax.optimization_barrier(
            (got_a[:early], got_b[:early], (got_a[anchor], got_b[anchor]))
        )
        got_a = list(held_a) + got_a[early:]
        got_b = list(held_b) + got_b[early:]

        rows_out = hidden.shape[0]
        side = lax.axis_index("tp")
        n_tp = rows_dev // rows_out

        def half(got, limits, lo, hi, which):
            q3 = queries.reshape(n_tp, rows_out, queries.shape[1])
            q3 = jnp.take(q3, which, axis=0)[:, lo * HEAD : hi * HEAD]
            q3 = q3.reshape(rows_out, hi - lo, HEAD).transpose(1, 0, 2)
            parts = []
            for first, last in phases:
                stack = jnp.stack(got[first:last])
                keys = stack[:, : hi - lo]
                values = stack[:, hi - lo :]
                keeping = within[None, :] < limits[first:last, None]
                parts.append(attend_part(q3, keys, values, keeping, scale_factor))
            return combine(parts, rows_out)

        def attention_rows(which):
            return jnp.concatenate(
                [half(got_a, limit_a, 0, heads_a, which), half(got_b, limit_b, heads_a, heads_here, which)],
                axis=1,
            )

        other = jnp.dot(attention_rows(1 - side), out_weight, preferred_element_type=jnp.float32)
        other = other.astype(jnp.bfloat16)
        came = lax.ppermute(other, "tp", [(0, 1), (1, 0)])
        attention_own = attention_rows(side)
        own = jnp.dot(attention_own, out_weight, preferred_element_type=jnp.float32)
        own = lax.optimization_barrier(own)
        summed = own + came.astype(jnp.float32)
        return (hidden.astype(jnp.float32) + gate_scale * summed).astype(jnp.bfloat16)

    placed = (
        P(("seq", "tp"), None),
        P("seq", "tp"),
        P("seq", "tp"),
        P("seq", "tp"),
        P(),
        P("tp", None),
        P("seq"),
        P("seq"),
    )
    return jax.shard_map(
        on_device, mesh=mesh, in_specs=placed, out_specs=P(("seq", "tp"), None), check_vma=False
    )
```

```python
import math

import jax
import jax.numpy as jnp
from jax import lax
from jax.sharding import PartitionSpec as P

HEAD = 128
neg_large = -1e30


def snake_ring(chips):
    half = chips // 2
    return [2 * a for a in range(half)] + [2 * a + 1 for a in reversed(range(half))]


def build(n_seq):
    chips = n_seq // 2
    ring = snake_ring(chips)
    half = chips // 2
    forward = [(ring[p] * 2 + c, ring[(p + 1) % chips] * 2 + c) for p in range(chips) for c in range(2)]
    backward = [(ring[(p + 1) % chips] * 2 + c, ring[p] * 2 + c) for p in range(chips) for c in range(2)]
    swap = [(i, i ^ 1) for i in range(n_seq)]

    def chip_at(pos):
        return jnp.where(pos < half, 2 * pos, 2 * (chips - 1 - pos) + 1)

    def gather_ring(packet_a, packet_b, me):
        chip = me // 2
        core = me % 2
        pos = jnp.where(chip % 2 == 0, chip // 2, chips - 1 - chip // 2)
        ring_a, ring_b = [packet_a], [packet_b]
        for step in range(1, chips):
            ring_a.append(lax.ppermute(ring_a[-1], "seq", forward))
            ring_b.append(lax.ppermute(ring_b[-1], "seq", backward))
        got_a, got_b, ids_a, ids_b = [], [], [], []
        for step in range(chips):
            cur_a, cur_b = ring_a[step], ring_b[step]
            if step + 1 < chips:
                cur_a, _ = lax.optimization_barrier((cur_a, ring_a[step + 1]))
                cur_b, _ = lax.optimization_barrier((cur_b, ring_b[step + 1]))
            src_a = chip_at((pos - step) % chips) * 2 + core
            src_b = chip_at((pos + step) % chips) * 2 + core
            got_a += [ring_a[step], lax.ppermute(cur_a, "seq", swap)]
            got_b += [ring_b[step], lax.ppermute(cur_b, "seq", swap)]
            ids_a += [src_a, src_a ^ 1]
            ids_b += [src_b, src_b ^ 1]
        return got_a, got_b, jnp.stack(ids_a), jnp.stack(ids_b)

    return gather_ring


def attend_part(queries_3d, keys, values, keeping, scale_factor):
    scores = (
        jnp.einsum("hqd,nhkd->hqnk", queries_3d, keys, preferred_element_type=jnp.float32)
        * scale_factor
    )
    masked = jnp.where(keeping[None, None], scores, neg_large)
    peak = jnp.max(masked, axis=(2, 3))[:, :, None]
    weights = jnp.where(keeping[None, None], jnp.exp(masked - peak[:, :, :, None]), 0.0)
    totals = jnp.sum(weights, axis=(2, 3))[:, :, None]
    summed = jnp.einsum(
        "hqnk,nhkd->hqd", weights.astype(jnp.bfloat16), values, preferred_element_type=jnp.float32
    )
    return peak, totals, summed


def combine(parts, rows_dev):
    peak = parts[0][0]
    for part in parts[1:]:
        peak = jnp.maximum(peak, part[0])
    totals = 0.0
    summed = 0.0
    for part_peak, part_totals, part_summed in parts:
        factor = jnp.exp(part_peak - peak)
        totals = totals + factor * part_totals
        summed = summed + factor * part_summed
    result = (summed / totals).astype(jnp.bfloat16)
    return result.transpose(1, 0, 2).reshape(rows_dev, -1)


def solution(mesh):
    n_seq = mesh.shape["seq"]
    gather_ring = build(n_seq)

    def on_device(
        hidden, queries, key_rows, value_rows, gate_scale, out_weight, valid_count, assignment
    ):
        rows_dev = queries.shape[0]
        heads_here = queries.shape[1] // HEAD
        heads_a = heads_here // 2
        cut = heads_a * HEAD
        scale_factor = 1.0 / math.sqrt(HEAD)
        me = lax.axis_index("seq")
        rows_pad = (rows_dev + 1 + 7) // 8 * 8
        row_id = lax.broadcasted_iota(jnp.int32, (rows_pad - rows_dev, HEAD), 0)
        col_id = lax.broadcasted_iota(jnp.int32, (rows_pad - rows_dev, HEAD), 1)
        info = jnp.where(
            (row_id == 0) & (col_id == 0),
            valid_count[0],
            jnp.where((row_id == 0) & (col_id == 1), assignment[0], 0),
        ).astype(jnp.bfloat16)

        def head_major(lo, hi):
            both = jnp.concatenate([key_rows[:, lo * HEAD : hi * HEAD], value_rows[:, lo * HEAD : hi * HEAD]], axis=1)
            both = both.reshape(rows_dev, 2 * (hi - lo), HEAD).transpose(1, 0, 2)
            pad = jnp.broadcast_to(info[None], (2 * (hi - lo),) + info.shape)
            return jnp.concatenate([both, pad], axis=1)

        packet_a = head_major(0, heads_a)
        packet_b = head_major(heads_a, heads_here)
        got_a, got_b, ids_a, ids_b = gather_ring(packet_a, packet_b, me)
        chips = n_seq // 2
        known = chips // 2
        seen = 2 * (known + 1)
        heard = got_a[:seen] + got_b[:seen]
        heard_ids = jnp.concatenate([ids_a[:seen], ids_b[:seen]])
        extra = jnp.stack([g[0, rows_dev, :2] for g in heard]).astype(jnp.float32).astype(jnp.int32)
        counts_of, blocks_of = extra[:, 0], extra[:, 1]

        def limits_for(ids):
            clip = jnp.max(jnp.where(ids[:, None] == heard_ids[None, :], blocks_of[None, :], -1), axis=1)
            return jnp.max(jnp.where(clip[:, None] == heard_ids[None, :], counts_of[None, :], -1), axis=1)

        limit_a = limits_for(ids_a)
        limit_b = limits_for(ids_b)
        within = jnp.arange(rows_pad, dtype=jnp.int32)
        phases = [(0, known + 1), (known + 1, chips - 1), (chips - 1, chips)]
        phases = [(2 * lo, 2 * hi) for lo, hi in phases if hi > lo]

        anchor = 2 * max(chips - 2, 0)
        early = 2 * (chips - 1)
        held_a, held_b, _ = lax.optimization_barrier(
            (got_a[:early], got_b[:early], (got_a[anchor], got_b[anchor]))
        )
        got_a = list(held_a) + got_a[early:]
        got_b = list(held_b) + got_b[early:]

        rows_out = hidden.shape[0]
        side = lax.axis_index("tp")
        n_tp = rows_dev // rows_out

        def half(got, limits, lo, hi, which):
            q3 = queries.reshape(n_tp, rows_out, queries.shape[1])
            q3 = jnp.take(q3, which, axis=0)[:, lo * HEAD : hi * HEAD]
            q3 = q3.reshape(rows_out, hi - lo, HEAD).transpose(1, 0, 2)
            parts = []
            for first, last in phases:
                stack = jnp.stack(got[first:last])
                keys = stack[:, : hi - lo]
                values = stack[:, hi - lo :]
                keeping = within[None, :] < limits[first:last, None]
                parts.append(attend_part(q3, keys, values, keeping, scale_factor))
            return combine(parts, rows_out)

        def attention_rows(which):
            return jnp.concatenate(
                [half(got_a, limit_a, 0, heads_a, which), half(got_b, limit_b, heads_a, heads_here, which)],
                axis=1,
            )

        other = jnp.dot(attention_rows(1 - side), out_weight, preferred_element_type=jnp.float32)
        other = other.astype(jnp.bfloat16)
        came = lax.ppermute(other, "tp", [(0, 1), (1, 0)])
        attention_own = attention_rows(side)
        own = jnp.dot(attention_own, out_weight, preferred_element_type=jnp.float32)
        own = lax.optimization_barrier(own)
        summed = own + came.astype(jnp.float32)
        return (hidden.astype(jnp.float32) + gate_scale * summed).astype(jnp.bfloat16)

    placed = (
        P(("seq", "tp"), None),
        P("seq", "tp"),
        P("seq", "tp"),
        P("seq", "tp"),
        P(),
        P("tp", None),
        P("seq"),
        P("seq"),
    )
    return jax.shard_map(
        on_device, mesh=mesh, in_specs=placed, out_specs=P(("seq", "tp"), None), check_vma=False
    )
```

```python
import math

import jax
import jax.numpy as jnp
from jax import lax
from jax.sharding import PartitionSpec as P

HEAD = 128
neg_large = -1e30


def snake_ring(chips):
    half = chips // 2
    return [2 * a for a in range(half)] + [2 * a + 1 for a in reversed(range(half))]


def build(n_seq):
    chips = n_seq // 2
    ring = snake_ring(chips)
    half = chips // 2
    forward = [(ring[p] * 2 + c, ring[(p + 1) % chips] * 2 + c) for p in range(chips) for c in range(2)]
    backward = [(ring[(p + 1) % chips] * 2 + c, ring[p] * 2 + c) for p in range(chips) for c in range(2)]
    swap = [(i, i ^ 1) for i in range(n_seq)]

    def chip_at(pos):
        return jnp.where(pos < half, 2 * pos, 2 * (chips - 1 - pos) + 1)

    def gather_ring(packet_a, packet_b, me):
        chip = me // 2
        core = me % 2
        pos = jnp.where(chip % 2 == 0, chip // 2, chips - 1 - chip // 2)
        ring_a, ring_b = [packet_a], [packet_b]
        for step in range(1, chips):
            ring_a.append(lax.ppermute(ring_a[-1], "seq", forward))
            ring_b.append(lax.ppermute(ring_b[-1], "seq", backward))
        got_a, got_b, ids_a, ids_b = [], [], [], []
        for step in range(chips):
            cur_a, cur_b = ring_a[step], ring_b[step]
            if step == 0 and chips > 1:
                cur_a, cur_b, _ = lax.optimization_barrier((cur_a, cur_b, (ring_a[1], ring_b[1])))
            src_a = chip_at((pos - step) % chips) * 2 + core
            src_b = chip_at((pos + step) % chips) * 2 + core
            got_a += [ring_a[step], lax.ppermute(cur_a, "seq", swap)]
            got_b += [ring_b[step], lax.ppermute(cur_b, "seq", swap)]
            ids_a += [src_a, src_a ^ 1]
            ids_b += [src_b, src_b ^ 1]
        return got_a, got_b, jnp.stack(ids_a), jnp.stack(ids_b)

    return gather_ring


def attend_part(queries_3d, keys, values, keeping, scale_factor):
    scores = (
        jnp.einsum("hqd,nhkd->hqnk", queries_3d, keys, preferred_element_type=jnp.float32)
        * scale_factor
    )
    masked = jnp.where(keeping[None, None], scores, neg_large)
    peak = jnp.max(masked, axis=(2, 3))[:, :, None]
    weights = jnp.where(keeping[None, None], jnp.exp(masked - peak[:, :, :, None]), 0.0)
    totals = jnp.sum(weights, axis=(2, 3))[:, :, None]
    summed = jnp.einsum(
        "hqnk,nhkd->hqd", weights.astype(jnp.bfloat16), values, preferred_element_type=jnp.float32
    )
    return peak, totals, summed


def combine(parts, rows_dev):
    peak = parts[0][0]
    for part in parts[1:]:
        peak = jnp.maximum(peak, part[0])
    totals = 0.0
    summed = 0.0
    for part_peak, part_totals, part_summed in parts:
        factor = jnp.exp(part_peak - peak)
        totals = totals + factor * part_totals
        summed = summed + factor * part_summed
    result = (summed / totals).astype(jnp.bfloat16)
    return result.transpose(1, 0, 2).reshape(rows_dev, -1)


def solution(mesh):
    n_seq = mesh.shape["seq"]
    gather_ring = build(n_seq)

    def on_device(
        hidden, queries, key_rows, value_rows, gate_scale, out_weight, valid_count, assignment
    ):
        rows_dev = queries.shape[0]
        heads_here = queries.shape[1] // HEAD
        heads_a = heads_here // 2
        cut = heads_a * HEAD
        scale_factor = 1.0 / math.sqrt(HEAD)
        me = lax.axis_index("seq")
        rows_pad = (rows_dev + 1 + 7) // 8 * 8
        row_id = lax.broadcasted_iota(jnp.int32, (rows_pad - rows_dev, HEAD), 0)
        col_id = lax.broadcasted_iota(jnp.int32, (rows_pad - rows_dev, HEAD), 1)
        info = jnp.where(
            (row_id == 0) & (col_id == 0),
            valid_count[0],
            jnp.where((row_id == 0) & (col_id == 1), assignment[0], 0),
        ).astype(jnp.bfloat16)

        def head_major(lo, hi):
            both = jnp.concatenate([key_rows[:, lo * HEAD : hi * HEAD], value_rows[:, lo * HEAD : hi * HEAD]], axis=1)
            both = both.reshape(rows_dev, 2 * (hi - lo), HEAD).transpose(1, 0, 2)
            pad = jnp.broadcast_to(info[None], (2 * (hi - lo),) + info.shape)
            return jnp.concatenate([both, pad], axis=1)

        packet_a = head_major(0, heads_a)
        packet_b = head_major(heads_a, heads_here)
        got_a, got_b, ids_a, ids_b = gather_ring(packet_a, packet_b, me)
        chips = n_seq // 2
        known = chips // 2
        seen = 2 * (known + 1)
        heard = got_a[:seen] + got_b[:seen]
        heard_ids = jnp.concatenate([ids_a[:seen], ids_b[:seen]])
        extra = jnp.stack([g[0, rows_dev, :2] for g in heard]).astype(jnp.float32).astype(jnp.int32)
        counts_of, blocks_of = extra[:, 0], extra[:, 1]

        def limits_for(ids):
            clip = jnp.max(jnp.where(ids[:, None] == heard_ids[None, :], blocks_of[None, :], -1), axis=1)
            return jnp.max(jnp.where(clip[:, None] == heard_ids[None, :], counts_of[None, :], -1), axis=1)

        limit_a = limits_for(ids_a)
        limit_b = limits_for(ids_b)
        within = jnp.arange(rows_pad, dtype=jnp.int32)
        phases = [(0, known + 1), (known + 1, chips - 1), (chips - 1, chips)]
        phases = [(2 * lo, 2 * hi) for lo, hi in phases if hi > lo]

        anchor = 2 * max(chips - 2, 0)
        early = 2 * (chips - 1)
        held_a, held_b, _ = lax.optimization_barrier(
            (got_a[:early], got_b[:early], (got_a[anchor], got_b[anchor]))
        )
        got_a = list(held_a) + got_a[early:]
        got_b = list(held_b) + got_b[early:]

        rows_out = hidden.shape[0]
        side = lax.axis_index("tp")
        n_tp = rows_dev // rows_out

        def half(got, limits, lo, hi, which):
            q3 = queries.reshape(n_tp, rows_out, queries.shape[1])
            q3 = jnp.take(q3, which, axis=0)[:, lo * HEAD : hi * HEAD]
            q3 = q3.reshape(rows_out, hi - lo, HEAD).transpose(1, 0, 2)
            parts = []
            for first, last in phases:
                stack = jnp.stack(got[first:last])
                keys = stack[:, : hi - lo]
                values = stack[:, hi - lo :]
                keeping = within[None, :] < limits[first:last, None]
                parts.append(attend_part(q3, keys, values, keeping, scale_factor))
            return combine(parts, rows_out)

        def attention_rows(which):
            return jnp.concatenate(
                [half(got_a, limit_a, 0, heads_a, which), half(got_b, limit_b, heads_a, heads_here, which)],
                axis=1,
            )

        other = jnp.dot(attention_rows(1 - side), out_weight, preferred_element_type=jnp.float32)
        other = other.astype(jnp.bfloat16)
        came = lax.ppermute(other, "tp", [(0, 1), (1, 0)])
        attention_own = attention_rows(side)
        own = jnp.dot(attention_own, out_weight, preferred_element_type=jnp.float32)
        own = lax.optimization_barrier(own)
        summed = own + came.astype(jnp.float32)
        return (hidden.astype(jnp.float32) + gate_scale * summed).astype(jnp.bfloat16)

    placed = (
        P(("seq", "tp"), None),
        P("seq", "tp"),
        P("seq", "tp"),
        P("seq", "tp"),
        P(),
        P("tp", None),
        P("seq"),
        P("seq"),
    )
    return jax.shard_map(
        on_device, mesh=mesh, in_specs=placed, out_specs=P(("seq", "tp"), None), check_vma=False
    )
```

```python
import math

import jax
import jax.numpy as jnp
from jax import lax
from jax.sharding import PartitionSpec as P

HEAD = 128
neg_large = -1e30


def snake_ring(chips):
    half = chips // 2
    return [2 * a for a in range(half)] + [2 * a + 1 for a in reversed(range(half))]


def build(n_seq):
    chips = n_seq // 2
    ring = snake_ring(chips)
    half = chips // 2
    forward = [(ring[p] * 2 + c, ring[(p + 1) % chips] * 2 + c) for p in range(chips) for c in range(2)]
    backward = [(ring[(p + 1) % chips] * 2 + c, ring[p] * 2 + c) for p in range(chips) for c in range(2)]
    swap = [(i, i ^ 1) for i in range(n_seq)]

    def chip_at(pos):
        return jnp.where(pos < half, 2 * pos, 2 * (chips - 1 - pos) + 1)

    def gather_ring(packet_a, packet_b, me):
        chip = me // 2
        core = me % 2
        pos = jnp.where(chip % 2 == 0, chip // 2, chips - 1 - chip // 2)
        got_a, got_b, ids_a, ids_b = [], [], [], []
        cur_a, cur_b = packet_a, packet_b
        for step in range(chips):
            if step > 0:
                cur_a = lax.ppermute(cur_a, "seq", forward)
                cur_b = lax.ppermute(cur_b, "seq", backward)
            src_a = chip_at((pos - step) % chips) * 2 + core
            src_b = chip_at((pos + step) % chips) * 2 + core
            mate_a = lax.ppermute(cur_a, "seq", swap)
            mate_b = lax.ppermute(cur_b, "seq", swap)
            got_a += [cur_a, mate_a]
            got_b += [cur_b, mate_b]
            ids_a += [src_a, src_a ^ 1]
            ids_b += [src_b, src_b ^ 1]
        return got_a, got_b, jnp.stack(ids_a), jnp.stack(ids_b)

    return gather_ring


def attend_part(queries_3d, keys, values, keeping, scale_factor):
    scores = (
        jnp.einsum("hqd,nhkd->hqnk", queries_3d, keys, preferred_element_type=jnp.float32)
        * scale_factor
    )
    masked = jnp.where(keeping[None, None], scores, neg_large)
    peak = jnp.max(masked, axis=(2, 3))[:, :, None]
    weights = jnp.where(keeping[None, None], jnp.exp(masked - peak[:, :, :, None]), 0.0)
    totals = jnp.sum(weights, axis=(2, 3))[:, :, None]
    summed = jnp.einsum(
        "hqnk,nhkd->hqd", weights.astype(jnp.bfloat16), values, preferred_element_type=jnp.float32
    )
    return peak, totals, summed


def combine(parts, rows_dev):
    peak = parts[0][0]
    for part in parts[1:]:
        peak = jnp.maximum(peak, part[0])
    totals = 0.0
    summed = 0.0
    for part_peak, part_totals, part_summed in parts:
        factor = jnp.exp(part_peak - peak)
        totals = totals + factor * part_totals
        summed = summed + factor * part_summed
    result = (summed / totals).astype(jnp.bfloat16)
    return result.transpose(1, 0, 2).reshape(rows_dev, -1)


def solution(mesh):
    n_seq = mesh.shape["seq"]
    gather_ring = build(n_seq)

    def on_device(
        hidden, queries, key_rows, value_rows, gate_scale, out_weight, valid_count, assignment
    ):
        rows_dev = queries.shape[0]
        heads_here = queries.shape[1] // HEAD
        heads_a = heads_here // 2
        cut = heads_a * HEAD
        scale_factor = 1.0 / math.sqrt(HEAD)
        me = lax.axis_index("seq")
        rows_pad = (rows_dev + 1 + 7) // 8 * 8
        row_id = lax.broadcasted_iota(jnp.int32, (rows_pad - rows_dev, HEAD), 0)
        col_id = lax.broadcasted_iota(jnp.int32, (rows_pad - rows_dev, HEAD), 1)
        info = jnp.where(
            (row_id == 0) & (col_id == 0),
            valid_count[0],
            jnp.where((row_id == 0) & (col_id == 1), assignment[0], 0),
        ).astype(jnp.bfloat16)

        def head_major(lo, hi):
            both = jnp.concatenate([key_rows[:, lo * HEAD : hi * HEAD], value_rows[:, lo * HEAD : hi * HEAD]], axis=1)
            both = both.reshape(rows_dev, 2 * (hi - lo), HEAD).transpose(1, 0, 2)
            pad = jnp.broadcast_to(info[None], (2 * (hi - lo),) + info.shape)
            return jnp.concatenate([both, pad], axis=1)

        packet_a = head_major(0, heads_a)
        packet_b = head_major(heads_a, heads_here)
        got_a, got_b, ids_a, ids_b = gather_ring(packet_a, packet_b, me)
        chips = n_seq // 2
        known = chips // 2
        seen = 2 * (known + 1)
        heard = got_a[:seen] + got_b[:seen]
        heard_ids = jnp.concatenate([ids_a[:seen], ids_b[:seen]])
        extra = jnp.stack([g[0, rows_dev, :2] for g in heard]).astype(jnp.float32).astype(jnp.int32)
        counts_of, blocks_of = extra[:, 0], extra[:, 1]

        def limits_for(ids):
            clip = jnp.max(jnp.where(ids[:, None] == heard_ids[None, :], blocks_of[None, :], -1), axis=1)
            return jnp.max(jnp.where(clip[:, None] == heard_ids[None, :], counts_of[None, :], -1), axis=1)

        limit_a = limits_for(ids_a)
        limit_b = limits_for(ids_b)
        within = jnp.arange(rows_pad, dtype=jnp.int32)
        phases = [(0, known + 1), (known + 1, chips)]
        phases = [(2 * lo, 2 * hi) for lo, hi in phases if hi > lo]

        anchor = 2 * max(chips - 2, 0)
        early = 2 * (chips - 1)
        held_a, held_b, _ = lax.optimization_barrier(
            (got_a[:early], got_b[:early], (got_a[anchor], got_b[anchor]))
        )
        got_a = list(held_a) + got_a[early:]
        got_b = list(held_b) + got_b[early:]

        rows_out = hidden.shape[0]
        side = lax.axis_index("tp")
        n_tp = rows_dev // rows_out

        def half(got, limits, lo, hi, which):
            q3 = queries.reshape(n_tp, rows_out, queries.shape[1])
            q3 = jnp.take(q3, which, axis=0)[:, lo * HEAD : hi * HEAD]
            q3 = q3.reshape(rows_out, hi - lo, HEAD).transpose(1, 0, 2)
            parts = []
            for first, last in phases:
                stack = jnp.stack(got[first:last])
                keys = stack[:, : hi - lo]
                values = stack[:, hi - lo :]
                keeping = within[None, :] < limits[first:last, None]
                parts.append(attend_part(q3, keys, values, keeping, scale_factor))
            return combine(parts, rows_out)

        def attention_rows(which):
            return jnp.concatenate(
                [half(got_a, limit_a, 0, heads_a, which), half(got_b, limit_b, heads_a, heads_here, which)],
                axis=1,
            )

        other = jnp.dot(attention_rows(1 - side), out_weight, preferred_element_type=jnp.float32)
        other = other.astype(jnp.bfloat16)
        came = lax.ppermute(other, "tp", [(0, 1), (1, 0)])
        attention_own = attention_rows(side)
        own = jnp.dot(attention_own, out_weight, preferred_element_type=jnp.float32)
        own = lax.optimization_barrier(own)
        summed = own + came.astype(jnp.float32)
        return (hidden.astype(jnp.float32) + gate_scale * summed).astype(jnp.bfloat16)

    placed = (
        P(("seq", "tp"), None),
        P("seq", "tp"),
        P("seq", "tp"),
        P("seq", "tp"),
        P(),
        P("tp", None),
        P("seq"),
        P("seq"),
    )
    return jax.shard_map(
        on_device, mesh=mesh, in_specs=placed, out_specs=P(("seq", "tp"), None), check_vma=False
    )
```

```python
import math

import jax
import jax.numpy as jnp
from jax import lax
from jax.sharding import PartitionSpec as P

HEAD = 128
neg_large = -1e30


def snake_ring(chips):
    half = chips // 2
    return [2 * a for a in range(half)] + [2 * a + 1 for a in reversed(range(half))]


def build(n_seq):
    chips = n_seq // 2
    ring = snake_ring(chips)
    half = chips // 2
    forward = [(ring[p] * 2 + c, ring[(p + 1) % chips] * 2 + c) for p in range(chips) for c in range(2)]
    backward = [(ring[(p + 1) % chips] * 2 + c, ring[p] * 2 + c) for p in range(chips) for c in range(2)]
    swap = [(i, i ^ 1) for i in range(n_seq)]

    def chip_at(pos):
        return jnp.where(pos < half, 2 * pos, 2 * (chips - 1 - pos) + 1)

    def gather_ring(packet_a, packet_b, me):
        chip = me // 2
        core = me % 2
        pos = jnp.where(chip % 2 == 0, chip // 2, chips - 1 - chip // 2)
        got_a, got_b, ids_a, ids_b = [], [], [], []
        cur_a, cur_b = packet_a, packet_b
        for step in range(chips):
            if step > 0:
                cur_a = lax.ppermute(cur_a, "seq", forward)
                cur_b = lax.ppermute(cur_b, "seq", backward)
            src_a = chip_at((pos - step) % chips) * 2 + core
            src_b = chip_at((pos + step) % chips) * 2 + core
            mate_a = lax.ppermute(cur_a, "seq", swap)
            mate_b = lax.ppermute(cur_b, "seq", swap)
            got_a += [cur_a, mate_a]
            got_b += [cur_b, mate_b]
            ids_a += [src_a, src_a ^ 1]
            ids_b += [src_b, src_b ^ 1]
        return got_a, got_b, jnp.stack(ids_a), jnp.stack(ids_b)

    return gather_ring


def attend_part(queries_3d, keys, values, keeping, scale_factor):
    scores = (
        jnp.einsum("hqd,nhkd->hqnk", queries_3d, keys, preferred_element_type=jnp.float32)
        * scale_factor
    )
    masked = jnp.where(keeping[None, None], scores, neg_large)
    peak = jnp.max(masked, axis=(2, 3))[:, :, None]
    weights = jnp.where(keeping[None, None], jnp.exp(masked - peak[:, :, :, None]), 0.0)
    totals = jnp.sum(weights, axis=(2, 3))[:, :, None]
    summed = jnp.einsum(
        "hqnk,nhkd->hqd", weights.astype(jnp.bfloat16), values, preferred_element_type=jnp.float32
    )
    return peak, totals, summed


def combine(parts, rows_dev):
    peak = parts[0][0]
    for part in parts[1:]:
        peak = jnp.maximum(peak, part[0])
    totals = 0.0
    summed = 0.0
    for part_peak, part_totals, part_summed in parts:
        factor = jnp.exp(part_peak - peak)
        totals = totals + factor * part_totals
        summed = summed + factor * part_summed
    result = (summed / totals).astype(jnp.bfloat16)
    return result.transpose(1, 0, 2).reshape(rows_dev, -1)


def solution(mesh):
    n_seq = mesh.shape["seq"]
    gather_ring = build(n_seq)

    def on_device(
        hidden, queries, key_rows, value_rows, gate_scale, out_weight, valid_count, assignment
    ):
        rows_dev = queries.shape[0]
        heads_here = queries.shape[1] // HEAD
        heads_a = heads_here // 2
        cut = heads_a * HEAD
        scale_factor = 1.0 / math.sqrt(HEAD)
        me = lax.axis_index("seq")
        rows_pad = (rows_dev + 1 + 7) // 8 * 8
        row_id = lax.broadcasted_iota(jnp.int32, (rows_pad - rows_dev, HEAD), 0)
        col_id = lax.broadcasted_iota(jnp.int32, (rows_pad - rows_dev, HEAD), 1)
        info = jnp.where(
            (row_id == 0) & (col_id == 0),
            valid_count[0],
            jnp.where((row_id == 0) & (col_id == 1), assignment[0], 0),
        ).astype(jnp.bfloat16)

        def head_major(lo, hi):
            both = jnp.concatenate([key_rows[:, lo * HEAD : hi * HEAD], value_rows[:, lo * HEAD : hi * HEAD]], axis=1)
            both = both.reshape(rows_dev, 2 * (hi - lo), HEAD).transpose(1, 0, 2)
            pad = jnp.broadcast_to(info[None], (2 * (hi - lo),) + info.shape)
            return jnp.concatenate([both, pad], axis=1)

        packet_a = head_major(0, heads_a)
        packet_b = head_major(heads_a, heads_here)
        got_a, got_b, ids_a, ids_b = gather_ring(packet_a, packet_b, me)
        chips = n_seq // 2
        known = chips // 2
        seen = 2 * (known + 1)
        heard = got_a[:seen] + got_b[:seen]
        heard_ids = jnp.concatenate([ids_a[:seen], ids_b[:seen]])
        extra = jnp.stack([g[0, rows_dev, :2] for g in heard]).astype(jnp.float32).astype(jnp.int32)
        counts_of, blocks_of = extra[:, 0], extra[:, 1]

        def limits_for(ids):
            clip = jnp.max(jnp.where(ids[:, None] == heard_ids[None, :], blocks_of[None, :], -1), axis=1)
            return jnp.max(jnp.where(clip[:, None] == heard_ids[None, :], counts_of[None, :], -1), axis=1)

        limit_a = limits_for(ids_a)
        limit_b = limits_for(ids_b)
        within = jnp.arange(rows_pad, dtype=jnp.int32)
        phases = [(0, known + 1), (known + 1, chips - 1), (chips - 1, chips)]
        phases = [(2 * lo, 2 * hi) for lo, hi in phases if hi > lo]

        anchor = 2 * max(chips - 2, 0)
        early = 2 * (chips - 1)
        held_a, held_b, _ = lax.optimization_barrier(
            (got_a[:early], got_b[:early], (got_a[anchor], got_b[anchor]))
        )
        got_a = list(held_a) + got_a[early:]
        got_b = list(held_b) + got_b[early:]

        rows_out = hidden.shape[0]
        side = lax.axis_index("tp")
        n_tp = rows_dev // rows_out

        def half(got, limits, lo, hi, which):
            q3 = queries.reshape(n_tp, rows_out, queries.shape[1])
            q3 = jnp.take(q3, which, axis=0)[:, lo * HEAD : hi * HEAD]
            q3 = q3.reshape(rows_out, hi - lo, HEAD).transpose(1, 0, 2)
            parts = []
            for first, last in phases:
                stack = jnp.stack(got[first:last])
                keys = stack[:, : hi - lo]
                values = stack[:, hi - lo :]
                keeping = within[None, :] < limits[first:last, None]
                parts.append(attend_part(q3, keys, values, keeping, scale_factor))
            return combine(parts, rows_out)

        def attention_rows(which):
            return jnp.concatenate(
                [half(got_a, limit_a, 0, heads_a, which), half(got_b, limit_b, heads_a, heads_here, which)],
                axis=1,
            )

        attention_other = attention_rows(1 - side)
        width_all = out_weight.shape[1]
        n_cols = 2 if width_all % (2 * HEAD) == 0 else 1
        width = width_all // n_cols
        came = []
        for i in range(n_cols):
            other = jnp.dot(
                attention_other, out_weight[:, i * width : (i + 1) * width], preferred_element_type=jnp.float32
            ).astype(jnp.bfloat16)
            came.append(lax.ppermute(other, "tp", [(0, 1), (1, 0)]))
        came = jnp.concatenate(came, axis=1)
        attention_own = attention_rows(side)
        own = jnp.dot(attention_own, out_weight, preferred_element_type=jnp.float32)
        own = lax.optimization_barrier(own)
        summed = own + came.astype(jnp.float32)
        return (hidden.astype(jnp.float32) + gate_scale * summed).astype(jnp.bfloat16)

    placed = (
        P(("seq", "tp"), None),
        P("seq", "tp"),
        P("seq", "tp"),
        P("seq", "tp"),
        P(),
        P("tp", None),
        P("seq"),
        P("seq"),
    )
    return jax.shard_map(
        on_device, mesh=mesh, in_specs=placed, out_specs=P(("seq", "tp"), None), check_vma=False
    )
```
